32 devices in a mesh: ctx: 16 (over z, x, core), tp: 2 (over y).
Axes of the slice: x: 2, y: 2, z: 4, core: 2. Of those that a mesh axis runs over, the one named last changes fastest.
Arguments:
- queries: bfloat16 [2048, 4096], P('ctx', 'tp'), may hold values from -100 to 100
- keys: bfloat16 [2048, 1024], P('ctx', 'tp'), may hold values from -4.5 to 4.5
- values: bfloat16 [2048, 1024], P('ctx', 'tp'), may hold values from -6 to 6
- out_weight: bfloat16 [4096, 4096], P('tp'), may hold values from -1.5 to 1.5
- group_widths: int32 [8], replicated, may hold values from 1 to 8, 16 in all
- pad_tokens: int32 [8], replicated, may hold values from 0 to 127
Outputs:
- mixed: bfloat16 [2048, 4096], P('ctx', 'tp')
The draws below stay inside these ranges and needn't reach their ends.
Inputs may be any that keep to these rules, and one draw needn't show every extreme that they name: `group_widths`: the group widths add up to the number of ctx indices, and the widest is exactly 8.
All inputs are finite; a program needn't handle non-finite values.
Results may differ from the reference program's by a relative error of at most 0.015.
Values may be sent and summed in bfloat16 or wider, within the bound.
No kernel may reach another device: no remote copies, remote signals or barrier semaphores. Data moves between devices by JAX's collectives and lax.ppermute only.
A program may use at most 64 MiB of HBM per device.

```python
import math
import jax
import jax.numpy as jnp
import numpy as np
from jax import lax

D = 4096
QUERY_HEADS = 32
KEY_VALUE_HEADS = 8
HEAD_SIZE = 128
TOKENS_PER_GROUP = 128
PROMPTS = 8
MAXW = 8
PACKED_TOKENS = 2048
N_CTX = 16
N_TP = 2


def shared_keys(key):
    base_offset = jax.random.normal(jax.random.fold_in(key, 11), (PACKED_TOKENS, KEY_VALUE_HEADS * HEAD_SIZE), jnp.float32)
    return jnp.clip(base_offset, -4.5, 4.5)


def draw_keys(key, part):
    unrotated_keys = shared_keys(key)
    return unrotated_keys.astype(jnp.bfloat16)


def draw_queries(key, part):
    base_offset = jax.random.normal(jax.random.fold_in(key, 12), (PACKED_TOKENS, QUERY_HEADS * HEAD_SIZE), jnp.float32)
    base_offset = jnp.clip(base_offset, -4.5, 4.5)
    return base_offset.astype(jnp.bfloat16)


def set_ends(entries, rng, low, largest):
    index_at = [jax.random.randint(jax.random.fold_in(rng, axis), (), 0, length) for axis, length in enumerate(entries.shape)]
    longest = entries.shape.index(max(entries.shape))
    next_to = index_at[:longest] + [(index_at[longest] + 1) % entries.shape[longest]] + index_at[longest + 1:]
    return entries.at[tuple(index_at)].set(low).at[tuple(next_to)].set(largest)


def level_of(stream_key, extent, split, least, top_value):
    def one(dim, shards_of):
        heights = jax.random.uniform(jax.random.fold_in(jax.random.fold_in(stream_key, 6), dim), (shards_of,), jnp.float32, least / len(split), top_value / len(split))
        return jnp.repeat(jnp.exp(heights), extent[dim] // shards_of).reshape((-1,) + (1,) * (len(extent) - dim - 1))

    gain = one(*split[0])
    for cut in split[1:]:
        gain = gain * one(*cut)
    return gain


def length_profile(number_of, total, reach, slope):
    loads = [(1 << 20) // math.isqrt(rank ** slope) + 1 for rank in range(2, number_of + 1)]
    surplus, given = total - reach - (number_of - 1), [1] * (number_of - 1)
    while surplus > 0:
        free = [i for i in range(number_of - 1) if given[i] < reach]
        mass, budget = sum([loads[i] for i in free]), surplus
        for i in free:
            extra = min(reach - given[i], max(1, budget * loads[i] // mass), surplus)
            given[i] = given[i] + extra
            surplus = surplus - extra
    return np.array([reach] + given)


def uneven(own_key, count, total, reach, skew):
    if count == 2:
        one = jax.random.randint(own_key, (), max(1, total - reach), min(reach, total - 1) + 1)
        return jnp.stack([one, total - one])
    tallies = jnp.asarray(length_profile(count, total, reach, skew), jnp.int32)
    twos = (count - 1) // 2
    donor, sink = tallies[1:1 + 2 * twos:2], tallies[2:2 + 2 * twos:2]
    slack = jnp.minimum(donor - 1, reach - sink)
    shifted = jax.random.randint(jax.random.fold_in(own_key, 1), (twos,), 0, 1 << 20) % (slack + 1)
    tallies = tallies.at[1:1 + 2 * twos:2].set(donor - shifted).at[2:2 + 2 * twos:2].set(sink + shifted)
    return tallies[jax.random.permutation(jax.random.fold_in(own_key, 2), count)]


def bell_draw(rng, extent, width, limit, shards=(), held_as=jnp.bfloat16):
    entries = width * jax.random.normal(rng, extent, jnp.float32)
    if shards:
        entries = entries * level_of(rng, extent, shards, -0.22, 0.18)
    return jnp.clip(entries, -limit, limit).astype(held_as)


def setup_inputs(seed: int = 0) -> dict:
    streams_of = jax.random.split(jax.random.key(seed), 7)
    return {
        "queries": draw_queries(jax.random.fold_in(streams_of[6], 71), 0),
        "keys": draw_keys(jax.random.fold_in(streams_of[6], 71), 0),
        "values": bell_draw(streams_of[2], (PACKED_TOKENS, KEY_VALUE_HEADS * HEAD_SIZE), 1.0, 6.0, ((0, 16), (1, 2))),
        "out_weight": bell_draw(streams_of[3], (QUERY_HEADS * HEAD_SIZE, D), 0.25, 1.5, ((0, 2),)),
        "group_widths": uneven(streams_of[4], PROMPTS, N_CTX, MAXW, 1).astype(jnp.int32),
        "pad_tokens": set_ends(jax.random.randint(streams_of[5], (PROMPTS,), 0, TOKENS_PER_GROUP), jax.random.fold_in(streams_of[5], 1), 0, TOKENS_PER_GROUP - 1).astype(jnp.int32),
    }


def rotate(block, positions):
    count = block.shape[0]
    heads = block.shape[1] // HEAD_SIZE
    half = HEAD_SIZE // 2
    pieces = block.astype(jnp.float32).reshape(count, heads, 2, half)
    freqs = 500000.0 ** (-jnp.arange(half, dtype=jnp.float32) / half)
    angles = positions.astype(jnp.float32)[:, None] * freqs[None, :]
    cosine = jnp.cos(angles)[:, None, :]
    sine = jnp.sin(angles)[:, None, :]
    first = pieces[:, :, 0, :]
    second = pieces[:, :, 1, :]
    turned = jnp.stack([first * cosine - second * sine, second * cosine + first * sine], axis=2)
    return turned.reshape(count, heads * HEAD_SIZE).astype(jnp.bfloat16)

def accumulate(carry, query_tile_rows, key_segment, value_segment, query_pos, key_pos, length):
    running, totals, summed = carry
    scores = jnp.einsum('rkgd,nkd->kgrn', query_tile_rows.astype(jnp.float32), key_segment.astype(jnp.float32)) * (1.0 / math.sqrt(HEAD_SIZE))
    allowed = (key_pos[None, :] <= query_pos[:, None]) & (key_pos[None, :] < length) & (key_pos[None, :] >= 0)
    scores = jnp.where(allowed, scores, -1e+30)
    highest = jnp.maximum(running, lax.optimization_barrier(jnp.max(scores, axis=-1)))
    weights = jnp.where(allowed, jnp.exp(scores - highest[..., None]), 0.0)
    factor = jnp.exp(running - highest)
    totals = totals * factor + lax.optimization_barrier(jnp.sum(weights, axis=-1))
    rounded = lax.optimization_barrier(weights.astype(jnp.bfloat16)).astype(jnp.float32)
    summed = summed * factor[..., None] + jnp.einsum('kgrn,nkd->kgrd', rounded, value_segment.astype(jnp.float32))
    return (highest, totals, summed)

def reference(queries, keys, values, out_weight, group_widths, pad_tokens):
    offsets = jnp.cumsum(group_widths) - group_widths
    shard_ids = jnp.arange(N_CTX, dtype=jnp.int32)
    owner = lax.optimization_barrier(jnp.sum((offsets[None, :] <= shard_ids[:, None]).astype(jnp.int32), axis=1)) - 1
    shard_start = offsets[owner]
    shard_length = group_widths[owner] * TOKENS_PER_GROUP - pad_tokens[owner]
    token_rows = jnp.arange(PACKED_TOKENS, dtype=jnp.int32)
    positions = token_rows - shard_start[token_rows // TOKENS_PER_GROUP] * TOKENS_PER_GROUP
    rotated_query_rows = rotate(queries, positions)
    rotated_key_rows = rotate(keys, positions)
    context_group = QUERY_HEADS // KEY_VALUE_HEADS
    local_rows = jnp.arange(TOKENS_PER_GROUP, dtype=jnp.int32)

    def one_shard(group_index):
        start = shard_start[group_index]
        length = shard_length[group_index]
        query_tile_rows = lax.dynamic_slice_in_dim(rotated_query_rows, (group_index * TOKENS_PER_GROUP).astype(jnp.int32), TOKENS_PER_GROUP, 0).reshape(TOKENS_PER_GROUP, KEY_VALUE_HEADS, context_group, HEAD_SIZE)
        query_pos = (group_index - start) * TOKENS_PER_GROUP + local_rows
        initial_state = (jnp.full((KEY_VALUE_HEADS, context_group, TOKENS_PER_GROUP), -1e+30, jnp.float32), jnp.zeros((KEY_VALUE_HEADS, context_group, TOKENS_PER_GROUP), jnp.float32), jnp.zeros((KEY_VALUE_HEADS, context_group, TOKENS_PER_GROUP, HEAD_SIZE), jnp.float32))

        def visit(carry, step):
            source = group_index - step

            def take(state):
                begin_offset = (source * TOKENS_PER_GROUP).astype(jnp.int32)
                key_segment = lax.dynamic_slice_in_dim(rotated_key_rows, begin_offset, TOKENS_PER_GROUP, 0).reshape(TOKENS_PER_GROUP, KEY_VALUE_HEADS, HEAD_SIZE)
                value_segment = lax.dynamic_slice_in_dim(values, begin_offset, TOKENS_PER_GROUP, 0).reshape(TOKENS_PER_GROUP, KEY_VALUE_HEADS, HEAD_SIZE)
                key_pos = (source - start) * TOKENS_PER_GROUP + local_rows
                return accumulate(state, query_tile_rows, key_segment, value_segment, query_pos, key_pos, length)

            def keep(state):
                return state
            return (lax.cond(source >= start, take, keep, carry), None)
        carry, _ = lax.scan(visit, initial_state, jnp.arange(MAXW, dtype=jnp.int32))
        running, totals, summed = carry
        result = summed / totals[..., None]
        return result.transpose(2, 0, 1, 3).reshape(TOKENS_PER_GROUP, QUERY_HEADS * HEAD_SIZE).astype(jnp.bfloat16)
    attended = lax.map(one_shard, shard_ids).reshape(PACKED_TOKENS, QUERY_HEADS * HEAD_SIZE)
    block = QUERY_HEADS * HEAD_SIZE // N_TP

    def add_block(total, number):
        begin_offset = (number * block).astype(jnp.int32)
        columns = lax.dynamic_slice_in_dim(attended, begin_offset, block, 1)
        weight_rows = lax.dynamic_slice_in_dim(out_weight, begin_offset, block, 0)
        partial_sum = jnp.dot(columns, weight_rows, preferred_element_type=jnp.float32)
        partial_sum = lax.optimization_barrier(partial_sum.astype(jnp.bfloat16)).astype(jnp.float32)
        return (total + partial_sum, None)
    total, _ = lax.scan(add_block, jnp.zeros((PACKED_TOKENS, D), jnp.float32), jnp.arange(N_TP, dtype=jnp.int32))
    return total.astype(jnp.bfloat16)
```

```python
import math

import jax
import jax.numpy as jnp
from jax import lax
from jax.sharding import PartitionSpec as P

HEAD_SIZE = 128
FAR = 1 << 20


def rotate(block, positions):
    count = block.shape[0]
    heads = block.shape[1] // HEAD_SIZE
    half = HEAD_SIZE // 2
    pieces = block.astype(jnp.float32).reshape(count, heads, 2, half)
    freqs = 500000.0 ** (-jnp.arange(half, dtype=jnp.float32) / half)
    angles = positions.astype(jnp.float32)[:, None] * freqs[None, :]
    cosine = jnp.cos(angles)[:, None, :]
    sine = jnp.sin(angles)[:, None, :]
    first = pieces[:, :, 0, :]
    second = pieces[:, :, 1, :]
    turned = jnp.stack([first * cosine - second * sine, second * cosine + first * sine], axis=2)
    return turned.reshape(count, heads * HEAD_SIZE).astype(jnp.bfloat16)


def gather_window(kv, n, window):
    received = []
    for s in range(1, window, 2):
        if s == 1:
            pairs = [(j, j + 1) for j in range(1, n - 1, 2)]
        else:
            pairs = [(j, j + s) for j in range(n - s)]
        received.append(lax.ppermute(kv, "ctx", pairs))
    core = lax.axis_index("ctx") % 2
    to_odd = jnp.stack([kv] + received[:-1])
    to_even = jnp.stack(received[1:] + [kv])
    outgoing = jnp.where(core == 0, to_odd, to_even)
    incoming = lax.ppermute(outgoing, "ctx", [(j, j ^ 1) for j in range(n)])
    slots = jnp.concatenate([kv[None], jnp.stack(received), incoming], axis=0)
    half = window // 2
    even_shift = [0] + [2 * m + 1 for m in range(half)] + [2 * m + 2 for m in range(half - 1)] + [FAR]
    odd_shift = [0, FAR] + [2 * m + 1 for m in range(1, half)] + [1] + [2 * m for m in range(1, half)]
    shift = jnp.where(core == 0, jnp.array(even_shift, jnp.int32), jnp.array(odd_shift, jnp.int32))
    return slots, shift


def on_device(queries, keys, values, out_weight, group_widths, pad_tokens):
    n = lax.axis_size("ctx")
    window = n // 2
    group_index = lax.axis_index("ctx")
    rows_here = queries.shape[0]
    heads_kv = keys.shape[1] // HEAD_SIZE
    context_group = queries.shape[1] // keys.shape[1]

    slots, shift = gather_window(jnp.stack([keys, values]), n, window)

    prompt_ids = jnp.arange(group_widths.shape[0], dtype=jnp.int32)
    offsets = jnp.sum(
        jnp.where(prompt_ids[None, :] < prompt_ids[:, None], group_widths[None, :], 0), axis=1
    )
    owner = jnp.sum((offsets <= group_index).astype(jnp.int32)) - 1
    picked = prompt_ids == owner
    start = jnp.sum(jnp.where(picked, offsets, 0))
    width = jnp.sum(jnp.where(picked, group_widths, 0))
    padding = jnp.sum(jnp.where(picked, pad_tokens, 0))
    length = width * rows_here - padding
    local_rows = jnp.arange(rows_here, dtype=jnp.int32)
    query_pos = (group_index - start) * rows_here + local_rows
    key_pos = ((group_index - shift - start) * rows_here)[:, None] + local_rows[None, :]
    key_pos = key_pos.reshape(-1)

    count = slots.shape[0] * rows_here
    query_rows = rotate(queries, query_pos).reshape(rows_here, heads_kv, context_group, HEAD_SIZE)
    key_rows = rotate(slots[:, 0].reshape(count, -1), key_pos).reshape(count, heads_kv, HEAD_SIZE)
    value_rows = slots[:, 1].reshape(count, heads_kv, HEAD_SIZE)

    scores = jnp.einsum(
        "rkgd,nkd->kgrn", query_rows, key_rows, preferred_element_type=jnp.float32
    ) * (1.0 / math.sqrt(HEAD_SIZE))
    allowed = (
        (key_pos[None, :] <= query_pos[:, None])
        & (key_pos[None, :] < length)
        & (key_pos[None, :] >= 0)
    )
    scores = jnp.where(allowed, scores, -1e30)
    highest = jnp.max(scores, axis=-1)
    weights = jnp.where(allowed, jnp.exp(scores - highest[..., None]), 0.0)
    totals = jnp.sum(weights, axis=-1)
    summed = jnp.einsum(
        "kgrn,nkd->kgrd", weights.astype(jnp.bfloat16), value_rows, preferred_element_type=jnp.float32
    )
    attended = (
        (summed / totals[..., None]).transpose(2, 0, 1, 3).reshape(rows_here, -1).astype(jnp.bfloat16)
    )

    n_tp = lax.axis_size("tp")
    if n_tp == 2:
        me = lax.axis_index("tp")
        part = out_weight.shape[1] // 2
        peer_weight = lax.dynamic_slice_in_dim(out_weight, (1 - me) * part, part, 1)
        peer_terms = jnp.dot(attended, peer_weight, preferred_element_type=jnp.float32)
        got = lax.ppermute(peer_terms.astype(jnp.bfloat16), "tp", [(0, 1), (1, 0)])
        own_weight = lax.dynamic_slice_in_dim(out_weight, me * part, part, 1)
        own_terms = jnp.dot(attended, own_weight, preferred_element_type=jnp.float32)
        own_terms = own_terms.astype(jnp.bfloat16).astype(jnp.float32)
        return (own_terms + got.astype(jnp.float32)).astype(jnp.bfloat16)
    terms = jnp.dot(attended, out_weight, preferred_element_type=jnp.float32)
    return lax.psum_scatter(terms.astype(jnp.bfloat16), "tp", scatter_dimension=1, tiled=True)


def solution(mesh):
    return jax.shard_map(
        on_device,
        mesh=mesh,
        in_specs=(P("ctx", "tp"), P("ctx", "tp"), P("ctx", "tp"), P("tp", None), P(), P()),
        out_specs=P("ctx", "tp"),
        check_vma=False,
    )
```

```python
import math

import jax
import jax.numpy as jnp
from jax import lax
from jax.experimental import pallas as pl
from jax.experimental.pallas import tpu as pltpu
from jax.sharding import PartitionSpec as P

HEAD_SIZE = 128
FAR = 1 << 20


def rotate(block, positions):
    count = block.shape[0]
    heads = block.shape[1] // HEAD_SIZE
    half = HEAD_SIZE // 2
    pieces = block.astype(jnp.float32).reshape(count, heads, 2, half)
    freqs = 500000.0 ** (-jnp.arange(half, dtype=jnp.float32) / half)
    angles = positions.astype(jnp.float32)[:, None] * freqs[None, :]
    cosine = jnp.cos(angles)[:, None, :]
    sine = jnp.sin(angles)[:, None, :]
    first = pieces[:, :, 0, :]
    second = pieces[:, :, 1, :]
    turned = jnp.stack([first * cosine - second * sine, second * cosine + first * sine], axis=2)
    return turned.reshape(count, heads * HEAD_SIZE).astype(jnp.bfloat16)


def gather_window(kv, n, window):
    received = []
    for s in range(1, window, 2):
        if s == 1:
            pairs = [(j, j + 1) for j in range(1, n - 1, 2)]
        else:
            pairs = [(j, j + s) for j in range(n - s)]
        received.append(lax.ppermute(kv, "ctx", pairs))
    core = lax.axis_index("ctx") % 2
    to_odd = jnp.stack([kv] + received[:-1])
    to_even = jnp.stack(received[1:] + [kv])
    outgoing = jnp.where(core == 0, to_odd, to_even)
    incoming = lax.ppermute(outgoing, "ctx", [(j, j ^ 1) for j in range(n)])
    slots = jnp.concatenate([kv[None], jnp.stack(received), incoming], axis=0)
    half = window // 2
    even_shift = [0] + [2 * m + 1 for m in range(half)] + [2 * m + 2 for m in range(half - 1)] + [FAR]
    odd_shift = [0, FAR] + [2 * m + 1 for m in range(1, half)] + [1] + [2 * m for m in range(1, half)]
    shift = jnp.where(core == 0, jnp.array(even_shift, jnp.int32), jnp.array(odd_shift, jnp.int32))
    return slots, shift


def attention_kernel(query_pos_ref, key_limit_ref, query_ref, key_ref, value_ref, out_ref):
    keys = key_ref[...]
    values = value_ref[...].reshape(keys.shape[0], HEAD_SIZE)
    allowed = key_limit_ref[...] <= query_pos_ref[...]
    for g in range(query_ref.shape[1] // HEAD_SIZE):
        columns = slice(g * HEAD_SIZE, (g + 1) * HEAD_SIZE)
        scores = lax.dot_general(
            query_ref[:, columns], keys, (((1,), (1,)), ((), ())), preferred_element_type=jnp.float32
        ) * (1.0 / math.sqrt(HEAD_SIZE))
        scores = jnp.where(allowed, scores, -1e30)
        highest = jnp.max(scores, axis=1, keepdims=True)
        weights = jnp.where(allowed, jnp.exp(scores - highest), 0.0)
        totals = jnp.sum(weights, axis=1, keepdims=True)
        summed = jnp.dot(weights.astype(jnp.bfloat16), values, preferred_element_type=jnp.float32)
        out_ref[:, columns] = (summed / totals).astype(out_ref.dtype)


def attend(query_pos, key_limit, query_rows, key_rows, slots, heads_kv):
    rows, width = query_rows.shape
    count = key_rows.shape[0]
    group = width // heads_kv
    n_slots = slots.shape[0]
    flops = 4 * rows * count * width
    return pl.pallas_call(
        attention_kernel,
        out_shape=jax.ShapeDtypeStruct((rows, width), jnp.bfloat16),
        grid=(heads_kv,),
        in_specs=[
            pl.BlockSpec((rows, 1), lambda h: (0, 0)),
            pl.BlockSpec((1, count), lambda h: (0, 0)),
            pl.BlockSpec((rows, group), lambda h: (0, h)),
            pl.BlockSpec((count, HEAD_SIZE), lambda h: (0, h)),
            pl.BlockSpec((n_slots, None, slots.shape[2], HEAD_SIZE), lambda h: (0, 1, 0, h)),
        ],
        out_specs=pl.BlockSpec((rows, group), lambda h: (0, h)),
        cost_estimate=pl.CostEstimate(
            flops=flops, transcendentals=rows * count * width // HEAD_SIZE,
            bytes_accessed=2 * (2 * rows * width + 2 * count * heads_kv * HEAD_SIZE),
        ),
    )(query_pos, key_limit, query_rows, key_rows, slots)


def on_device(queries, keys, values, out_weight, group_widths, pad_tokens):
    n = lax.axis_size("ctx")
    window = n // 2
    group_index = lax.axis_index("ctx")
    rows_here = queries.shape[0]
    heads_kv = keys.shape[1] // HEAD_SIZE
    context_group = queries.shape[1] // keys.shape[1]

    slots, shift = gather_window(jnp.stack([keys, values]), n, window)

    prompt_ids = jnp.arange(group_widths.shape[0], dtype=jnp.int32)
    offsets = jnp.sum(
        jnp.where(prompt_ids[None, :] < prompt_ids[:, None], group_widths[None, :], 0), axis=1
    )
    owner = jnp.sum((offsets <= group_index).astype(jnp.int32)) - 1
    picked = prompt_ids == owner
    start = jnp.sum(jnp.where(picked, offsets, 0))
    width = jnp.sum(jnp.where(picked, group_widths, 0))
    padding = jnp.sum(jnp.where(picked, pad_tokens, 0))
    length = width * rows_here - padding
    local_rows = jnp.arange(rows_here, dtype=jnp.int32)
    query_pos = (group_index - start) * rows_here + local_rows
    key_pos = ((group_index - shift - start) * rows_here)[:, None] + local_rows[None, :]
    key_pos = key_pos.reshape(-1)

    count = slots.shape[0] * rows_here
    query_rows = rotate(queries, query_pos)
    key_rows = rotate(slots[:, 0].reshape(count, -1), key_pos)
    usable = (key_pos >= 0) & (key_pos < length)
    key_limit = jnp.where(usable, key_pos, FAR * rows_here).reshape(1, count)
    attended = attend(query_pos.reshape(rows_here, 1), key_limit, query_rows, key_rows, slots, heads_kv)

    n_tp = lax.axis_size("tp")
    if n_tp == 2:
        me = lax.axis_index("tp")
        part = out_weight.shape[1] // 2
        peer_weight = lax.dynamic_slice_in_dim(out_weight, (1 - me) * part, part, 1)
        peer_terms = jnp.dot(attended, peer_weight, preferred_element_type=jnp.float32)
        got = lax.ppermute(peer_terms.astype(jnp.bfloat16), "tp", [(0, 1), (1, 0)])
        own_weight = lax.dynamic_slice_in_dim(out_weight, me * part, part, 1)
        own_terms = jnp.dot(attended, own_weight, preferred_element_type=jnp.float32)
        own_terms = lax.optimization_barrier(own_terms.astype(jnp.bfloat16)).astype(jnp.float32)
        return (own_terms + got.astype(jnp.float32)).astype(jnp.bfloat16)
    terms = jnp.dot(attended, out_weight, preferred_element_type=jnp.float32)
    return lax.psum_scatter(terms.astype(jnp.bfloat16), "tp", scatter_dimension=1, tiled=True)


def solution(mesh):
    return jax.shard_map(
        on_device,
        mesh=mesh,
        in_specs=(P("ctx", "tp"), P("ctx", "tp"), P("ctx", "tp"), P("tp", None), P(), P()),
        out_specs=P("ctx", "tp"),
        check_vma=False,
    )
```

```python
import math

import jax
import jax.numpy as jnp
from jax import lax
from jax.experimental import pallas as pl
from jax.experimental.pallas import tpu as pltpu
from jax.sharding import PartitionSpec as P

HEAD_SIZE = 128
FAR = 1 << 20


def gather_window(kv, n, window):
    received = []
    for s in range(1, window, 2):
        if s == 1:
            pairs = [(j, j + 1) for j in range(1, n - 1, 2)]
        else:
            pairs = [(j, j + s) for j in range(n - s)]
        received.append(lax.ppermute(kv, "ctx", pairs))
    core = lax.axis_index("ctx") % 2
    to_odd = jnp.stack([kv] + received[:-1])
    to_even = jnp.stack(received[1:] + [kv])
    outgoing = jnp.where(core == 0, to_odd, to_even)
    incoming = lax.ppermute(outgoing, "ctx", [(j, j ^ 1) for j in range(n)])
    slots = jnp.concatenate([kv[None], jnp.stack(received), incoming], axis=0)
    half = window // 2
    even_shift = [0] + [2 * m + 1 for m in range(half)] + [2 * m + 2 for m in range(half - 1)] + [FAR]
    odd_shift = [0, FAR] + [2 * m + 1 for m in range(1, half)] + [1] + [2 * m for m in range(1, half)]
    shift = jnp.where(core == 0, jnp.array(even_shift, jnp.int32), jnp.array(odd_shift, jnp.int32))
    return slots, shift


def turn(rows, cosine, sine):
    rows = rows.astype(jnp.float32)
    return (rows * cosine + pltpu.roll(rows, HEAD_SIZE // 2, 1) * sine).astype(jnp.bfloat16)


def attention_kernel(
    query_pos_ref, key_limit_ref, query_cos_ref, query_sin_ref, key_cos_ref, key_sin_ref,
    query_ref, key_ref, value_ref, out_ref,
):
    count = key_ref.shape[0] * key_ref.shape[1]
    keys = turn(key_ref[...].reshape(count, HEAD_SIZE), key_cos_ref[...], key_sin_ref[...])
    values = value_ref[...].reshape(count, HEAD_SIZE)
    allowed = key_limit_ref[...] <= query_pos_ref[...]
    for g in range(query_ref.shape[1] // HEAD_SIZE):
        columns = slice(g * HEAD_SIZE, (g + 1) * HEAD_SIZE)
        query = turn(query_ref[:, columns], query_cos_ref[...], query_sin_ref[...])
        scores = lax.dot_general(
            query, keys, (((1,), (1,)), ((), ())), preferred_element_type=jnp.float32
        ) * (1.0 / math.sqrt(HEAD_SIZE))
        scores = jnp.where(allowed, scores, -1e30)
        highest = jnp.max(scores, axis=1, keepdims=True)
        weights = jnp.exp(scores - highest)
        totals = jnp.sum(weights, axis=1, keepdims=True)
        summed = jnp.dot(weights.astype(jnp.bfloat16), values, preferred_element_type=jnp.float32)
        out_ref[:, columns] = (summed / totals).astype(out_ref.dtype)


def tables(positions):
    half = HEAD_SIZE // 2
    freqs = 500000.0 ** (-jnp.arange(half, dtype=jnp.float32) / half)
    angles = positions.astype(jnp.float32)[:, None] * freqs[None, :]
    cosine = jnp.cos(angles)
    sine = jnp.sin(angles)
    return jnp.concatenate([cosine, cosine], axis=1), jnp.concatenate([-sine, sine], axis=1)


def attend(query_pos, key_pos, key_limit, queries, slots, heads_kv):
    rows, width = queries.shape
    n_slots, _, block, _ = slots.shape
    count = n_slots * block
    group = width // heads_kv
    query_cos, query_sin = tables(query_pos)
    key_cos, key_sin = tables(key_pos)
    whole = lambda h: (0, 0)
    return pl.pallas_call(
        attention_kernel,
        out_shape=jax.ShapeDtypeStruct((rows, width), jnp.bfloat16),
        grid=(heads_kv,),
        in_specs=[
            pl.BlockSpec((rows, 1), whole),
            pl.BlockSpec((1, count), whole),
            pl.BlockSpec((rows, HEAD_SIZE), whole),
            pl.BlockSpec((rows, HEAD_SIZE), whole),
            pl.BlockSpec((count, HEAD_SIZE), whole),
            pl.BlockSpec((count, HEAD_SIZE), whole),
            pl.BlockSpec((rows, group), lambda h: (0, h)),
            pl.BlockSpec((n_slots, None, block, HEAD_SIZE), lambda h: (0, 0, 0, h)),
            pl.BlockSpec((n_slots, None, block, HEAD_SIZE), lambda h: (0, 1, 0, h)),
        ],
        out_specs=pl.BlockSpec((rows, group), lambda h: (0, h)),
        cost_estimate=pl.CostEstimate(
            flops=4 * rows * count * width, transcendentals=rows * count * width // HEAD_SIZE,
            bytes_accessed=2 * (2 * rows * width + 2 * count * heads_kv * HEAD_SIZE),
        ),
    )(query_pos.reshape(rows, 1), key_limit, query_cos, query_sin, key_cos, key_sin, queries, slots, slots)


def on_device(queries, keys, values, out_weight, group_widths, pad_tokens):
    n = lax.axis_size("ctx")
    window = n // 2
    group_index = lax.axis_index("ctx")
    rows_here = queries.shape[0]
    heads_kv = keys.shape[1] // HEAD_SIZE
    context_group = queries.shape[1] // keys.shape[1]

    slots, shift = gather_window(jnp.stack([keys, values]), n, window)

    prompt_ids = jnp.arange(group_widths.shape[0], dtype=jnp.int32)
    offsets = jnp.sum(
        jnp.where(prompt_ids[None, :] < prompt_ids[:, None], group_widths[None, :], 0), axis=1
    )
    owner = jnp.sum((offsets <= group_index).astype(jnp.int32)) - 1
    picked = prompt_ids == owner
    start = jnp.sum(jnp.where(picked, offsets, 0))
    width = jnp.sum(jnp.where(picked, group_widths, 0))
    padding = jnp.sum(jnp.where(picked, pad_tokens, 0))
    length = width * rows_here - padding
    local_rows = jnp.arange(rows_here, dtype=jnp.int32)
    query_pos = (group_index - start) * rows_here + local_rows
    key_pos = ((group_index - shift - start) * rows_here)[:, None] + local_rows[None, :]
    key_pos = key_pos.reshape(-1)

    usable = (key_pos >= 0) & (key_pos < length)
    key_limit = jnp.where(usable, key_pos, FAR * rows_here).reshape(1, -1)
    attended = attend(query_pos, key_pos, key_limit, queries, slots, heads_kv)

    n_tp = lax.axis_size("tp")
    if n_tp == 2:
        me = lax.axis_index("tp")
        part = out_weight.shape[1] // 2
        peer_weight = lax.dynamic_slice_in_dim(out_weight, (1 - me) * part, part, 1)
        peer_terms = jnp.dot(attended, peer_weight, preferred_element_type=jnp.float32)
        got = lax.ppermute(peer_terms.astype(jnp.bfloat16), "tp", [(0, 1), (1, 0)])
        own_weight = lax.dynamic_slice_in_dim(out_weight, me * part, part, 1)
        own_terms = jnp.dot(attended, own_weight, preferred_element_type=jnp.float32)
        own_terms = lax.optimization_barrier(own_terms.astype(jnp.bfloat16)).astype(jnp.float32)
        return (own_terms + got.astype(jnp.float32)).astype(jnp.bfloat16)
    terms = jnp.dot(attended, out_weight, preferred_element_type=jnp.float32)
    return lax.psum_scatter(terms.astype(jnp.bfloat16), "tp", scatter_dimension=1, tiled=True)


def solution(mesh):
    return jax.shard_map(
        on_device,
        mesh=mesh,
        in_specs=(P("ctx", "tp"), P("ctx", "tp"), P("ctx", "tp"), P("tp", None), P(), P()),
        out_specs=P("ctx", "tp"),
        check_vma=False,
    )
```

```python
import functools
import math

import jax
import jax.numpy as jnp
from jax import lax
from jax.experimental import pallas as pl
from jax.experimental.pallas import tpu as pltpu
from jax.sharding import PartitionSpec as P

HEAD_SIZE = 128
FAR = 1 << 20


def gather_window(kv, n, window):
    received = []
    for s in range(1, window, 2):
        if s == 1:
            pairs = [(j, j + 1) for j in range(1, n - 1, 2)]
        else:
            pairs = [(j, j + s) for j in range(n - s)]
        received.append(lax.ppermute(kv, "ctx", pairs))
    across = [(j, j ^ 1) for j in range(n)]
    passed = [lax.ppermute(block, "ctx", across) for block in [kv] + received]
    half = window // 2
    even_shift = [0] + [2 * m + 1 for m in range(half)] + [FAR, FAR] + [2 * m for m in range(1, half)]
    odd_shift = [0, FAR] + [2 * m + 1 for m in range(1, half)] + [1] + [2 * m + 2 for m in range(half)]
    core = lax.axis_index("ctx") % 2
    shift = jnp.where(core == 0, jnp.array(even_shift, jnp.int32), jnp.array(odd_shift, jnp.int32))
    return [kv] + received + passed, shift


def turn(rows, cosine, sine):
    rows = rows.astype(jnp.float32)
    return (rows * cosine + pltpu.roll(rows, HEAD_SIZE // 2, 1) * sine).astype(jnp.bfloat16)


def attention_kernel(n_slots, project, peer_ref, query_pos_ref, key_limit_ref, query_cos_ref, query_sin_ref,
                     key_cos_ref, key_sin_ref, query_ref, *refs):
    key_refs = refs[:n_slots]
    value_refs = refs[n_slots:2 * n_slots]
    keys = turn(jnp.concatenate([r[...] for r in key_refs], axis=0), key_cos_ref[...], key_sin_ref[...])
    values = jnp.concatenate([r[...] for r in value_refs], axis=0)
    allowed = key_limit_ref[...] <= query_pos_ref[...]
    out_ref = refs[2 * n_slots + 1] if project else refs[2 * n_slots]
    for g in range(query_ref.shape[1] // HEAD_SIZE):
        columns = slice(g * HEAD_SIZE, (g + 1) * HEAD_SIZE)
        query = turn(query_ref[:, columns], query_cos_ref[...], query_sin_ref[...])
        scores = lax.dot_general(
            query, keys, (((1,), (1,)), ((), ())), preferred_element_type=jnp.float32
        ) * (1.0 / math.sqrt(HEAD_SIZE))
        scores = jnp.where(allowed, scores, -1e30)
        highest = jnp.max(scores, axis=1, keepdims=True)
        weights = jnp.exp(scores - highest)
        totals = jnp.sum(weights, axis=1, keepdims=True)
        summed = jnp.dot(weights.astype(jnp.bfloat16), values, preferred_element_type=jnp.float32)
        out_ref[:, columns] = (summed / totals).astype(out_ref.dtype)
    if project:
        weight_ref = refs[2 * n_slots]
        peer_out_ref, total_ref = refs[2 * n_slots + 2], refs[2 * n_slots + 3]
        step = pl.program_id(0)

        @pl.when(step == 0)
        def _():
            total_ref[...] = jnp.zeros_like(total_ref)

        total_ref[...] += jnp.dot(out_ref[...], weight_ref[...], preferred_element_type=jnp.float32)

        @pl.when(step == pl.num_programs(0) - 1)
        def _():
            peer_out_ref[...] = total_ref[...].astype(peer_out_ref.dtype)


def tables(positions):
    half = HEAD_SIZE // 2
    freqs = 500000.0 ** (-jnp.arange(half, dtype=jnp.float32) / half)
    angles = positions.astype(jnp.float32)[:, None] * freqs[None, :]
    cosine = jnp.cos(angles)
    sine = jnp.sin(angles)
    return jnp.concatenate([cosine, cosine], axis=1), jnp.concatenate([-sine, sine], axis=1)


def attend(query_pos, key_pos, key_limit, queries, slots, heads_kv, out_weight, peer):
    rows, width = queries.shape
    block = slots[0].shape[1]
    n_slots = len(slots)
    count = n_slots * block
    group = width // heads_kv
    project = out_weight is not None
    query_cos, query_sin = tables(query_pos)
    key_cos, key_sin = tables(key_pos)
    whole = lambda h, p: (0, 0)
    in_specs = [
        pl.BlockSpec((rows, 1), whole),
        pl.BlockSpec((1, count), whole),
        pl.BlockSpec((rows, HEAD_SIZE), whole),
        pl.BlockSpec((rows, HEAD_SIZE), whole),
        pl.BlockSpec((count, HEAD_SIZE), whole),
        pl.BlockSpec((count, HEAD_SIZE), whole),
        pl.BlockSpec((rows, group), lambda h, p: (0, h)),
    ]
    in_specs += [pl.BlockSpec((None, block, HEAD_SIZE), lambda h, p: (0, 0, h))] * n_slots
    in_specs += [pl.BlockSpec((None, block, HEAD_SIZE), lambda h, p: (1, 0, h))] * n_slots
    out_shape = [jax.ShapeDtypeStruct((rows, width), jnp.bfloat16)]
    out_specs = [pl.BlockSpec((rows, group), lambda h, p: (0, h))]
    scratch = []
    args = [peer.reshape(1), query_pos.reshape(rows, 1), key_limit, query_cos, query_sin, key_cos, key_sin,
            queries] + slots + slots
    flops = 4 * rows * count * width
    moved = 2 * (2 * rows * width + 2 * count * heads_kv * HEAD_SIZE)
    if project:
        part = out_weight.shape[1] // 2
        in_specs.append(pl.BlockSpec((group, part), lambda h, p: (h, p[0])))
        out_shape.append(jax.ShapeDtypeStruct((rows, part), jnp.bfloat16))
        out_specs.append(pl.BlockSpec((rows, part), whole))
        scratch.append(pltpu.VMEM((rows, part), jnp.float32))
        args.append(out_weight)
        flops += 2 * rows * width * part
        moved += 2 * (width * part + rows * part)
    return pl.pallas_call(
        functools.partial(attention_kernel, n_slots, project),
        out_shape=out_shape,
        grid_spec=pltpu.PrefetchScalarGridSpec(
            num_scalar_prefetch=1, grid=(heads_kv,), in_specs=in_specs, out_specs=out_specs,
            scratch_shapes=scratch,
        ),
        cost_estimate=pl.CostEstimate(
            flops=flops, transcendentals=rows * count * width // HEAD_SIZE, bytes_accessed=moved
        ),
    )(*args)


def on_device(queries, keys, values, out_weight, group_widths, pad_tokens):
    n = lax.axis_size("ctx")
    window = n // 2
    group_index = lax.axis_index("ctx")
    rows_here = queries.shape[0]
    heads_kv = keys.shape[1] // HEAD_SIZE
    context_group = queries.shape[1] // keys.shape[1]

    slots, shift = gather_window(jnp.stack([keys, values]), n, window)

    prompt_ids = jnp.arange(group_widths.shape[0], dtype=jnp.int32)
    offsets = jnp.sum(
        jnp.where(prompt_ids[None, :] < prompt_ids[:, None], group_widths[None, :], 0), axis=1
    )
    owner = jnp.sum((offsets <= group_index).astype(jnp.int32)) - 1
    picked = prompt_ids == owner
    start = jnp.sum(jnp.where(picked, offsets, 0))
    width = jnp.sum(jnp.where(picked, group_widths, 0))
    padding = jnp.sum(jnp.where(picked, pad_tokens, 0))
    length = width * rows_here - padding
    local_rows = jnp.arange(rows_here, dtype=jnp.int32)
    query_pos = (group_index - start) * rows_here + local_rows
    key_pos = ((group_index - shift - start) * rows_here)[:, None] + local_rows[None, :]
    key_pos = key_pos.reshape(-1)

    usable = (key_pos >= 0) & (key_pos < length)
    key_limit = jnp.where(usable, key_pos, FAR * rows_here).reshape(1, -1)

    n_tp = lax.axis_size("tp")
    if n_tp == 2:
        me = lax.axis_index("tp")
        attended, peer_terms = attend(
            query_pos, key_pos, key_limit, queries, slots, heads_kv, out_weight, 1 - me
        )
        got = lax.ppermute(peer_terms, "tp", [(0, 1), (1, 0)])
        part = out_weight.shape[1] // 2
        own_weight = lax.dynamic_slice_in_dim(out_weight, me * part, part, 1)
        own_terms = jnp.dot(attended, own_weight, preferred_element_type=jnp.float32)
        own_terms = lax.optimization_barrier(own_terms.astype(jnp.bfloat16)).astype(jnp.float32)
        return (own_terms + got.astype(jnp.float32)).astype(jnp.bfloat16)
    (attended,) = attend(query_pos, key_pos, key_limit, queries, slots, heads_kv, None, jnp.int32(0))
    terms = jnp.dot(attended, out_weight, preferred_element_type=jnp.float32)
    return lax.psum_scatter(terms.astype(jnp.bfloat16), "tp", scatter_dimension=1, tiled=True)


def solution(mesh):
    return jax.shard_map(
        on_device,
        mesh=mesh,
        in_specs=(P("ctx", "tp"), P("ctx", "tp"), P("ctx", "tp"), P("tp", None), P(), P()),
        out_specs=P("ctx", "tp"),
        check_vma=False,
    )
```

```python
import functools
import math

import jax
import jax.numpy as jnp
from jax import lax
from jax.experimental import pallas as pl
from jax.experimental.pallas import tpu as pltpu
from jax.sharding import PartitionSpec as P

HEAD_SIZE = 128
FAR = 1 << 20


def gather_window(kv, n, window):
    half = window // 2
    received = [None] * half
    for m in reversed(range(half)):
        s = 2 * m + 1
        if s == 1:
            pairs = [(j, j + 1) for j in range(1, n - 1, 2)]
        else:
            pairs = [(j, j + s) for j in range(n - s)]
        received[m] = lax.ppermute(kv, "ctx", pairs)
    up = [(j, j + 1) for j in range(0, n, 2)]
    down = [(j + 1, j) for j in range(0, n, 2)]
    passed = [lax.ppermute(kv, "ctx", up)]
    for m in range(half):
        pairs = (up if m < half - 1 else []) + (down if m > 0 else [])
        passed.append(lax.ppermute(received[m], "ctx", pairs))
    slots = [kv] + received + passed
    even_use = [0] + [1 + m for m in range(half)] + [2 + half + m for m in range(1, half)]
    odd_use = [0] + [1 + m for m in range(1, half)] + [1 + half] + [2 + half + m for m in range(half - 1)]
    even_shift = [0] + [2 * m + 1 for m in range(half)] + [2 * m for m in range(1, half)]
    odd_shift = [0] + [2 * m + 1 for m in range(1, half)] + [1] + [2 * m + 2 for m in range(half - 1)]
    core = lax.axis_index("ctx") % 2
    shift = jnp.where(core == 0, jnp.array(even_shift, jnp.int32), jnp.array(odd_shift, jnp.int32))
    return slots, (even_use, odd_use), shift


def turn(rows, cosine, sine):
    rows = rows.astype(jnp.float32)
    return (rows * cosine + pltpu.roll(rows, HEAD_SIZE // 2, 1) * sine).astype(jnp.bfloat16)


def attention_kernel(n_slots, uses, project, peer_ref, core_ref, query_pos_ref, key_limit_ref, query_cos_ref,
                     query_sin_ref, key_cos_ref, key_sin_ref, query_ref, *refs):
    key_refs = refs[:n_slots]
    value_refs = refs[n_slots:2 * n_slots]
    out_ref = refs[2 * n_slots + 1] if project else refs[2 * n_slots]

    def attend_with(use):
        keys = turn(jnp.concatenate([key_refs[j][...] for j in use], axis=0), key_cos_ref[...], key_sin_ref[...])
        values = jnp.concatenate([value_refs[j][...] for j in use], axis=0)
        allowed = key_limit_ref[...] <= query_pos_ref[...]
        for g in range(query_ref.shape[1] // HEAD_SIZE):
            columns = slice(g * HEAD_SIZE, (g + 1) * HEAD_SIZE)
            query = turn(query_ref[:, columns], query_cos_ref[...], query_sin_ref[...])
            scores = lax.dot_general(
                query, keys, (((1,), (1,)), ((), ())), preferred_element_type=jnp.float32
            ) * (1.0 / math.sqrt(HEAD_SIZE))
            scores = jnp.where(allowed, scores, -1e30)
            highest = jnp.max(scores, axis=1, keepdims=True)
            weights = jnp.exp(scores - highest)
            totals = jnp.sum(weights, axis=1, keepdims=True)
            summed = jnp.dot(weights.astype(jnp.bfloat16), values, preferred_element_type=jnp.float32)
            out_ref[:, columns] = (summed / totals).astype(out_ref.dtype)

    for parity, use in enumerate(uses):
        pl.when(core_ref[0] == parity)(functools.partial(attend_with, use))
    if project:
        weight_ref = refs[2 * n_slots]
        peer_out_ref, total_ref = refs[2 * n_slots + 2], refs[2 * n_slots + 3]
        step = pl.program_id(0)

        @pl.when(step == 0)
        def _():
            total_ref[...] = jnp.zeros_like(total_ref)

        total_ref[...] += jnp.dot(out_ref[...], weight_ref[...], preferred_element_type=jnp.float32)

        @pl.when(step == pl.num_programs(0) - 1)
        def _():
            peer_out_ref[...] = total_ref[...].astype(peer_out_ref.dtype)


def tables(positions):
    half = HEAD_SIZE // 2
    freqs = 500000.0 ** (-jnp.arange(half, dtype=jnp.float32) / half)
    angles = positions.astype(jnp.float32)[:, None] * freqs[None, :]
    cosine = jnp.cos(angles)
    sine = jnp.sin(angles)
    return jnp.concatenate([cosine, cosine], axis=1), jnp.concatenate([-sine, sine], axis=1)


def attend(query_pos, key_pos, key_limit, queries, slots, uses, heads_kv, out_weight, peer):
    rows, width = queries.shape
    block = slots[0].shape[1]
    n_slots = len(slots)
    count = len(uses[0]) * block
    group = width // heads_kv
    project = out_weight is not None
    query_cos, query_sin = tables(query_pos)
    key_cos, key_sin = tables(key_pos)
    whole = lambda h, p, c: (0, 0)
    in_specs = [
        pl.BlockSpec((rows, 1), whole),
        pl.BlockSpec((1, count), whole),
        pl.BlockSpec((rows, HEAD_SIZE), whole),
        pl.BlockSpec((rows, HEAD_SIZE), whole),
        pl.BlockSpec((count, HEAD_SIZE), whole),
        pl.BlockSpec((count, HEAD_SIZE), whole),
        pl.BlockSpec((rows, group), lambda h, p, c: (0, h)),
    ]
    in_specs += [pl.BlockSpec((None, block, HEAD_SIZE), lambda h, p, c: (0, 0, h))] * n_slots
    in_specs += [pl.BlockSpec((None, block, HEAD_SIZE), lambda h, p, c: (1, 0, h))] * n_slots
    out_shape = [jax.ShapeDtypeStruct((rows, width), jnp.bfloat16)]
    out_specs = [pl.BlockSpec((rows, group), lambda h, p, c: (0, h))]
    scratch = []
    core = (lax.axis_index("ctx") % 2).astype(jnp.int32)
    args = [peer.reshape(1), core.reshape(1), query_pos.reshape(rows, 1), key_limit, query_cos, query_sin, key_cos, key_sin,
            queries] + slots + slots
    flops = 4 * rows * count * width
    moved = 2 * (2 * rows * width + 2 * count * heads_kv * HEAD_SIZE)
    if project:
        part = out_weight.shape[1] // 2
        in_specs.append(pl.BlockSpec((group, part), lambda h, p, c: (h, p[0])))
        out_shape.append(jax.ShapeDtypeStruct((rows, part), jnp.bfloat16))
        out_specs.append(pl.BlockSpec((rows, part), whole))
        scratch.append(pltpu.VMEM((rows, part), jnp.float32))
        args.append(out_weight)
        flops += 2 * rows * width * part
        moved += 2 * (width * part + rows * part)
    return pl.pallas_call(
        functools.partial(attention_kernel, n_slots, uses, project),
        out_shape=out_shape,
        grid_spec=pltpu.PrefetchScalarGridSpec(
            num_scalar_prefetch=2, grid=(heads_kv,), in_specs=in_specs, out_specs=out_specs,
            scratch_shapes=scratch,
        ),
        cost_estimate=pl.CostEstimate(
            flops=flops, transcendentals=rows * count * width // HEAD_SIZE, bytes_accessed=moved
        ),
    )(*args)


def on_device(queries, keys, values, out_weight, group_widths, pad_tokens):
    n = lax.axis_size("ctx")
    window = n // 2
    group_index = lax.axis_index("ctx")
    rows_here = queries.shape[0]
    heads_kv = keys.shape[1] // HEAD_SIZE
    context_group = queries.shape[1] // keys.shape[1]

    slots, uses, shift = gather_window(jnp.stack([keys, values]), n, window)

    prompt_ids = jnp.arange(group_widths.shape[0], dtype=jnp.int32)
    offsets = jnp.sum(
        jnp.where(prompt_ids[None, :] < prompt_ids[:, None], group_widths[None, :], 0), axis=1
    )
    owner = jnp.sum((offsets <= group_index).astype(jnp.int32)) - 1
    picked = prompt_ids == owner
    start = jnp.sum(jnp.where(picked, offsets, 0))
    width = jnp.sum(jnp.where(picked, group_widths, 0))
    padding = jnp.sum(jnp.where(picked, pad_tokens, 0))
    length = width * rows_here - padding
    local_rows = jnp.arange(rows_here, dtype=jnp.int32)
    query_pos = (group_index - start) * rows_here + local_rows
    key_pos = ((group_index - shift - start) * rows_here)[:, None] + local_rows[None, :]
    key_pos = key_pos.reshape(-1)

    usable = (key_pos >= 0) & (key_pos < length)
    key_limit = jnp.where(usable, key_pos, FAR * rows_here).reshape(1, -1)

    n_tp = lax.axis_size("tp")
    if n_tp == 2:
        me = lax.axis_index("tp")
        attended, peer_terms = attend(
            query_pos, key_pos, key_limit, queries, slots, uses, heads_kv, out_weight, 1 - me
        )
        got = lax.ppermute(peer_terms, "tp", [(0, 1), (1, 0)])
        part = out_weight.shape[1] // 2
        own_weight = lax.dynamic_slice_in_dim(out_weight, me * part, part, 1)
        own_terms = jnp.dot(attended, own_weight, preferred_element_type=jnp.float32)
        own_terms = lax.optimization_barrier(own_terms.astype(jnp.bfloat16)).astype(jnp.float32)
        return (own_terms + got.astype(jnp.float32)).astype(jnp.bfloat16)
    (attended,) = attend(query_pos, key_pos, key_limit, queries, slots, uses, heads_kv, None, jnp.int32(0))
    terms = jnp.dot(attended, out_weight, preferred_element_type=jnp.float32)
    return lax.psum_scatter(terms.astype(jnp.bfloat16), "tp", scatter_dimension=1, tiled=True)


def solution(mesh):
    return jax.shard_map(
        on_device,
        mesh=mesh,
        in_specs=(P("ctx", "tp"), P("ctx", "tp"), P("ctx", "tp"), P("tp", None), P(), P()),
        out_specs=P("ctx", "tp"),
        check_vma=False,
    )
```

```python
import functools
import math

import jax
import jax.numpy as jnp
from jax import lax
from jax.experimental import pallas as pl
from jax.experimental.pallas import tpu as pltpu
from jax.sharding import PartitionSpec as P

HEAD_SIZE = 128
FAR = 1 << 20
CHUNK = 32


def gather_window(kv, n, window):
    half = window // 2
    received = [None] * half
    for m in reversed(range(half)):
        s = 2 * m + 1
        if s == 1:
            pairs = [(j, j + 1) for j in range(1, n - 1, 2)]
        else:
            pairs = [(j, j + s) for j in range(n - s)]
        received[m] = lax.ppermute(kv, "ctx", pairs)
    up = [(j, j + 1) for j in range(0, n, 2)]
    down = [(j + 1, j) for j in range(0, n, 2)]
    passed = [lax.ppermute(kv, "ctx", up)]
    for m in range(half):
        pairs = (up if m < half - 1 else []) + (down if m > 0 else [])
        passed.append(lax.ppermute(received[m], "ctx", pairs))
    slots = [kv] + received + passed
    even_use = [0] + [1 + m for m in range(half)] + [2 + half + m for m in range(1, half)]
    odd_use = [0] + [1 + m for m in range(1, half)] + [1 + half] + [2 + half + m for m in range(half - 1)]
    even_shift = [0] + [2 * m + 1 for m in range(half)] + [2 * m for m in range(1, half)]
    odd_shift = [0] + [2 * m + 1 for m in range(1, half)] + [1] + [2 * m + 2 for m in range(half - 1)]
    core = lax.axis_index("ctx") % 2
    shift = jnp.where(core == 0, jnp.array(even_shift, jnp.int32), jnp.array(odd_shift, jnp.int32))
    return slots, (even_use, odd_use), shift


def turn(rows, cosine, sine):
    rows = rows.astype(jnp.float32)
    return (rows * cosine + pltpu.roll(rows, HEAD_SIZE // 2, 1) * sine).astype(jnp.bfloat16)


def attention_kernel(n_slots, uses, project, peer_ref, core_ref, query_pos_ref, key_limit_ref, query_cos_ref,
                     query_sin_ref, key_cos_ref, key_sin_ref, query_ref, *refs):
    key_refs = refs[:n_slots]
    value_refs = refs[n_slots:2 * n_slots]
    rest = refs[2 * n_slots:]
    if project:
        weight_ref, out_ref, peer_out_ref, total_ref, keys_ref, values_ref = rest
    else:
        out_ref, keys_ref, values_ref = rest
    block = key_refs[0].shape[0]

    def fill(use):
        for j, slot in enumerate(use):
            rows = slice(j * block, (j + 1) * block)
            keys_ref[rows, :] = turn(key_refs[slot][...], key_cos_ref[rows, :], key_sin_ref[rows, :])
            values_ref[rows, :] = value_refs[slot][...]

    for parity, use in enumerate(uses):
        pl.when(core_ref[0] == parity)(functools.partial(fill, use))

    chunks = query_ref.shape[0] // CHUNK

    def one(step, carry):
        g, r = step // chunks, step % chunks
        rows = pl.ds(pl.multiple_of(r * CHUNK, CHUNK), CHUNK)
        columns = pl.ds(pl.multiple_of(g * HEAD_SIZE, HEAD_SIZE), HEAD_SIZE)
        query = turn(query_ref[rows, columns], query_cos_ref[rows, :], query_sin_ref[rows, :])
        scores = lax.dot_general(
            query, keys_ref[...], (((1,), (1,)), ((), ())), preferred_element_type=jnp.float32
        ) * (1.0 / math.sqrt(HEAD_SIZE))
        allowed = key_limit_ref[...] <= query_pos_ref[rows, :]
        scores = jnp.where(allowed, scores, -1e30)
        highest = jnp.max(scores, axis=1, keepdims=True)
        weights = jnp.exp(scores - highest)
        totals = jnp.sum(weights, axis=1, keepdims=True)
        summed = jnp.dot(weights.astype(jnp.bfloat16), values_ref[...], preferred_element_type=jnp.float32)
        out_ref[rows, columns] = (summed / totals).astype(out_ref.dtype)
        return carry

    lax.fori_loop(0, (query_ref.shape[1] // HEAD_SIZE) * chunks, one, 0)
    if project:
        step = pl.program_id(0)

        @pl.when(step == 0)
        def _():
            total_ref[...] = jnp.zeros_like(total_ref)

        total_ref[...] += jnp.dot(out_ref[...], weight_ref[...], preferred_element_type=jnp.float32)

        @pl.when(step == pl.num_programs(0) - 1)
        def _():
            peer_out_ref[...] = total_ref[...].astype(peer_out_ref.dtype)


def tables(positions):
    half = HEAD_SIZE // 2
    freqs = 500000.0 ** (-jnp.arange(half, dtype=jnp.float32) / half)
    angles = positions.astype(jnp.float32)[:, None] * freqs[None, :]
    cosine = jnp.cos(angles)
    sine = jnp.sin(angles)
    return jnp.concatenate([cosine, cosine], axis=1), jnp.concatenate([-sine, sine], axis=1)


def attend(query_pos, key_pos, key_limit, queries, slots, uses, heads_kv, out_weight, peer):
    rows, width = queries.shape
    block = slots[0].shape[1]
    n_slots = len(slots)
    count = len(uses[0]) * block
    group = width // heads_kv
    project = out_weight is not None
    query_cos, query_sin = tables(query_pos)
    key_cos, key_sin = tables(key_pos)
    whole = lambda h, p, c: (0, 0)
    in_specs = [
        pl.BlockSpec((rows, 1), whole),
        pl.BlockSpec((1, count), whole),
        pl.BlockSpec((rows, HEAD_SIZE), whole),
        pl.BlockSpec((rows, HEAD_SIZE), whole),
        pl.BlockSpec((count, HEAD_SIZE), whole),
        pl.BlockSpec((count, HEAD_SIZE), whole),
        pl.BlockSpec((rows, group), lambda h, p, c: (0, h)),
    ]
    in_specs += [pl.BlockSpec((None, block, HEAD_SIZE), lambda h, p, c: (0, 0, h))] * n_slots
    in_specs += [pl.BlockSpec((None, block, HEAD_SIZE), lambda h, p, c: (1, 0, h))] * n_slots
    out_shape = [jax.ShapeDtypeStruct((rows, width), jnp.bfloat16)]
    out_specs = [pl.BlockSpec((rows, group), lambda h, p, c: (0, h))]
    scratch = []
    core = (lax.axis_index("ctx") % 2).astype(jnp.int32)
    args = [peer.reshape(1), core.reshape(1), query_pos.reshape(rows, 1), key_limit, query_cos, query_sin, key_cos, key_sin,
            queries] + slots + slots
    flops = 4 * rows * count * width
    moved = 2 * (2 * rows * width + 2 * count * heads_kv * HEAD_SIZE)
    if project:
        part = out_weight.shape[1] // 2
        in_specs.append(pl.BlockSpec((group, part), lambda h, p, c: (h, p[0])))
        out_shape.append(jax.ShapeDtypeStruct((rows, part), jnp.bfloat16))
        out_specs.append(pl.BlockSpec((rows, part), whole))
        scratch.append(pltpu.VMEM((rows, part), jnp.float32))
        args.append(out_weight)
        flops += 2 * rows * width * part
        moved += 2 * (width * part + rows * part)
    scratch += [pltpu.VMEM((count, HEAD_SIZE), jnp.bfloat16), pltpu.VMEM((count, HEAD_SIZE), jnp.bfloat16)]
    return pl.pallas_call(
        functools.partial(attention_kernel, n_slots, uses, project),
        out_shape=out_shape,
        grid_spec=pltpu.PrefetchScalarGridSpec(
            num_scalar_prefetch=2, grid=(heads_kv,), in_specs=in_specs, out_specs=out_specs,
            scratch_shapes=scratch,
        ),
        cost_estimate=pl.CostEstimate(
            flops=flops, transcendentals=rows * count * width // HEAD_SIZE, bytes_accessed=moved
        ),
    )(*args)


def on_device(queries, keys, values, out_weight, group_widths, pad_tokens):
    n = lax.axis_size("ctx")
    window = n // 2
    group_index = lax.axis_index("ctx")
    rows_here = queries.shape[0]
    heads_kv = keys.shape[1] // HEAD_SIZE
    context_group = queries.shape[1] // keys.shape[1]

    slots, uses, shift = gather_window(jnp.stack([keys, values]), n, window)

    prompt_ids = jnp.arange(group_widths.shape[0], dtype=jnp.int32)
    offsets = jnp.sum(
        jnp.where(prompt_ids[None, :] < prompt_ids[:, None], group_widths[None, :], 0), axis=1
    )
    owner = jnp.sum((offsets <= group_index).astype(jnp.int32)) - 1
    picked = prompt_ids == owner
    start = jnp.sum(jnp.where(picked, offsets, 0))
    width = jnp.sum(jnp.where(picked, group_widths, 0))
    padding = jnp.sum(jnp.where(picked, pad_tokens, 0))
    length = width * rows_here - padding
    local_rows = jnp.arange(rows_here, dtype=jnp.int32)
    query_pos = (group_index - start) * rows_here + local_rows
    key_pos = ((group_index - shift - start) * rows_here)[:, None] + local_rows[None, :]
    key_pos = key_pos.reshape(-1)

    usable = (key_pos >= 0) & (key_pos < length)
    key_limit = jnp.where(usable, key_pos, FAR * rows_here).reshape(1, -1)

    n_tp = lax.axis_size("tp")
    if n_tp == 2:
        me = lax.axis_index("tp")
        attended, peer_terms = attend(
            query_pos, key_pos, key_limit, queries, slots, uses, heads_kv, out_weight, 1 - me
        )
        got = lax.ppermute(peer_terms, "tp", [(0, 1), (1, 0)])
        part = out_weight.shape[1] // 2
        own_weight = lax.dynamic_slice_in_dim(out_weight, me * part, part, 1)
        own_terms = jnp.dot(attended, own_weight, preferred_element_type=jnp.float32)
        own_terms = lax.optimization_barrier(own_terms.astype(jnp.bfloat16)).astype(jnp.float32)
        return (own_terms + got.astype(jnp.float32)).astype(jnp.bfloat16)
    (attended,) = attend(query_pos, key_pos, key_limit, queries, slots, uses, heads_kv, None, jnp.int32(0))
    terms = jnp.dot(attended, out_weight, preferred_element_type=jnp.float32)
    return lax.psum_scatter(terms.astype(jnp.bfloat16), "tp", scatter_dimension=1, tiled=True)


def solution(mesh):
    return jax.shard_map(
        on_device,
        mesh=mesh,
        in_specs=(P("ctx", "tp"), P("ctx", "tp"), P("ctx", "tp"), P("tp", None), P(), P()),
        out_specs=P("ctx", "tp"),
        check_vma=False,
    )
```

```python
import functools
import math

import jax
import jax.numpy as jnp
from jax import lax
from jax.experimental import pallas as pl
from jax.experimental.pallas import tpu as pltpu
from jax.sharding import PartitionSpec as P

HEAD_SIZE = 128
FAR = 1 << 20


def gather_window(kv, n, window):
    half = window // 2
    received = [None] * half
    for m in reversed(range(half)):
        s = 2 * m + 1
        if s == 1:
            pairs = [(j, j + 1) for j in range(1, n - 1, 2)]
        else:
            pairs = [(j, j + s) for j in range(n - s)]
        received[m] = lax.ppermute(kv, "ctx", pairs)
    up = [(j, j + 1) for j in range(0, n, 2)]
    down = [(j + 1, j) for j in range(0, n, 2)]
    passed = [lax.ppermute(kv, "ctx", up)]
    for m in range(half - 1):
        pairs = up + (down if m > 0 else [])
        passed.append(lax.ppermute(received[m], "ctx", pairs))
    slots = [kv] + received + passed

    def pass_last(block):
        return lax.ppermute(block, "ctx", down)
    even = [(0, 0)] + [(1 + m, 2 * m + 1) for m in range(half - 1)] + [(2 + half + m, 2 * m) for m in range(1, half - 1)]
    even += [(half, 2 * half - 1), (2 * half + 1, 2 * half - 2)]
    odd = [(0, 0)] + [(1 + m, 2 * m + 1) for m in range(1, half - 1)] + [(1 + half, 1)]
    odd += [(2 + half + m, 2 * m + 2) for m in range(half - 2)] + [(half, 2 * half - 1), (2 * half, 2 * half - 2)]
    return slots, (even, odd), pass_last


def turn(rows, cosine, sine):
    rows = rows.astype(jnp.float32)
    return (rows * cosine + pltpu.roll(rows, HEAD_SIZE // 2, 1) * sine).astype(jnp.bfloat16)


def scores_of(query_ref, query_cos_ref, query_sin_ref, keys, allowed, g):
    columns = slice(g * HEAD_SIZE, (g + 1) * HEAD_SIZE)
    query = turn(query_ref[:, columns], query_cos_ref[...], query_sin_ref[...])
    scores = lax.dot_general(
        query, keys, (((1,), (1,)), ((), ())), preferred_element_type=jnp.float32
    ) * (1.0 / math.sqrt(HEAD_SIZE))
    return columns, jnp.where(allowed, scores, -1e30)


def attention_kernel(n_slots, uses, late, project, peer_ref, core_ref, query_pos_ref, key_limit_ref, query_cos_ref,
                     query_sin_ref, key_cos_ref, key_sin_ref, query_ref, *refs):
    if late:
        acc_in_ref, max_in_ref, sum_in_ref = refs[:3]
        refs = refs[3:]
    key_refs = refs[:n_slots]
    value_refs = refs[n_slots:2 * n_slots]
    rest = refs[2 * n_slots:]

    def body(use):
        keys = turn(jnp.concatenate([key_refs[j][...] for j in use], axis=0), key_cos_ref[...], key_sin_ref[...])
        values = jnp.concatenate([value_refs[j][...] for j in use], axis=0)
        allowed = key_limit_ref[...] <= query_pos_ref[...]
        for g in range(query_ref.shape[1] // HEAD_SIZE):
            columns, scores = scores_of(query_ref, query_cos_ref, query_sin_ref, keys, allowed, g)
            highest = jnp.max(scores, axis=1, keepdims=True)
            if late:
                before = max_in_ref[:, g:g + 1]
                highest = jnp.maximum(before, highest)
                factor = jnp.exp(before - highest)
            weights = jnp.exp(scores - highest)
            totals = jnp.sum(weights, axis=1, keepdims=True)
            summed = jnp.dot(weights.astype(jnp.bfloat16), values, preferred_element_type=jnp.float32)
            if late:
                totals = sum_in_ref[:, g:g + 1] * factor + totals
                summed = acc_in_ref[:, columns] * factor + summed
                out_ref[:, columns] = (summed / totals).astype(out_ref.dtype)
            else:
                acc_ref[:, columns] = summed
                max_ref[:, g:g + 1] = highest
                sum_ref[:, g:g + 1] = totals

    if late:
        if project:
            weight_ref, out_ref, peer_out_ref, total_ref = rest
        else:
            (out_ref,) = rest
    else:
        acc_ref, max_ref, sum_ref = rest
    for parity, use in enumerate(uses):
        pl.when(core_ref[0] == parity)(functools.partial(body, use))
    if late and project:
        step = pl.program_id(0)

        @pl.when(step == 0)
        def _():
            total_ref[...] = jnp.zeros_like(total_ref)

        total_ref[...] += jnp.dot(out_ref[...], weight_ref[...], preferred_element_type=jnp.float32)

        @pl.when(step == pl.num_programs(0) - 1)
        def _():
            peer_out_ref[...] = total_ref[...].astype(peer_out_ref.dtype)


def tables(positions):
    half = HEAD_SIZE // 2
    freqs = 500000.0 ** (-jnp.arange(half, dtype=jnp.float32) / half)
    angles = positions.astype(jnp.float32)[:, None] * freqs[None, :]
    cosine = jnp.cos(angles)
    sine = jnp.sin(angles)
    return jnp.concatenate([cosine, cosine], axis=1), jnp.concatenate([-sine, sine], axis=1)


def attend_stage(place, queries, slots, chosen, heads_kv, carry=None, out_weight=None, peer=None):
    query_pos, key_position, length, core = place
    rows, width = queries.shape
    block = slots[0].shape[1]
    present = sorted({s for pairs in chosen for s, _ in pairs})
    uses = [[present.index(s) for s, _ in pairs] for pairs in chosen]
    shift = jnp.where(core == 0, *[jnp.array([t for _, t in pairs], jnp.int32) for pairs in chosen])
    key_pos = key_position(shift)
    usable = (key_pos >= 0) & (key_pos < length)
    key_limit = jnp.where(usable, key_pos, FAR * rows).reshape(1, -1)
    count = key_pos.shape[0]
    group = width // heads_kv
    heads_here = group // HEAD_SIZE
    late = carry is not None
    project = out_weight is not None
    query_cos, query_sin = tables(query_pos)
    key_cos, key_sin = tables(key_pos)
    whole = lambda h, p, c: (0, 0)
    by_head = lambda h, p, c: (0, h)
    stats = lambda h, p, c: (h, 0, 0)
    in_specs = [
        pl.BlockSpec((rows, 1), whole),
        pl.BlockSpec((1, count), whole),
        pl.BlockSpec((rows, HEAD_SIZE), whole),
        pl.BlockSpec((rows, HEAD_SIZE), whole),
        pl.BlockSpec((count, HEAD_SIZE), whole),
        pl.BlockSpec((count, HEAD_SIZE), whole),
        pl.BlockSpec((rows, group), by_head),
    ]
    args = [peer.reshape(1), core.astype(jnp.int32).reshape(1), query_pos.reshape(rows, 1), key_limit,
            query_cos, query_sin, key_cos, key_sin, queries]
    if late:
        in_specs += [pl.BlockSpec((rows, group), by_head), pl.BlockSpec((None, rows, heads_here), stats),
                     pl.BlockSpec((None, rows, heads_here), stats)]
        args += list(carry)
    picked = [slots[s] for s in present]
    in_specs += [pl.BlockSpec((None, block, HEAD_SIZE), lambda h, p, c: (0, 0, h))] * len(picked)
    in_specs += [pl.BlockSpec((None, block, HEAD_SIZE), lambda h, p, c: (1, 0, h))] * len(picked)
    args += picked + picked
    flops = 4 * rows * count * width
    moved = 2 * (2 * rows * width + 2 * count * heads_kv * HEAD_SIZE)
    scratch = []
    if late:
        out_shape = [jax.ShapeDtypeStruct((rows, width), jnp.bfloat16)]
        out_specs = [pl.BlockSpec((rows, group), by_head)]
        if project:
            part = out_weight.shape[1] // 2
            in_specs.append(pl.BlockSpec((group, part), lambda h, p, c: (h, p[0])))
            out_shape.append(jax.ShapeDtypeStruct((rows, part), jnp.bfloat16))
            out_specs.append(pl.BlockSpec((rows, part), whole))
            scratch.append(pltpu.VMEM((rows, part), jnp.float32))
            args.append(out_weight)
            flops += 2 * rows * width * part
            moved += 2 * (width * part + rows * part)
    else:
        out_shape = [jax.ShapeDtypeStruct((rows, width), jnp.float32),
                     jax.ShapeDtypeStruct((heads_kv, rows, heads_here), jnp.float32),
                     jax.ShapeDtypeStruct((heads_kv, rows, heads_here), jnp.float32)]
        out_specs = [pl.BlockSpec((rows, group), by_head), pl.BlockSpec((None, rows, heads_here), stats),
                     pl.BlockSpec((None, rows, heads_here), stats)]
    return pl.pallas_call(
        functools.partial(attention_kernel, len(picked), uses, late, project),
        out_shape=out_shape,
        grid_spec=pltpu.PrefetchScalarGridSpec(
            num_scalar_prefetch=2, grid=(heads_kv,), in_specs=in_specs, out_specs=out_specs,
            scratch_shapes=scratch,
        ),
        cost_estimate=pl.CostEstimate(
            flops=flops, transcendentals=rows * count * width // HEAD_SIZE, bytes_accessed=moved
        ),
    )(*args)


def on_device(queries, keys, values, out_weight, group_widths, pad_tokens):
    n = lax.axis_size("ctx")
    window = n // 2
    group_index = lax.axis_index("ctx")
    rows_here = queries.shape[0]
    heads_kv = keys.shape[1] // HEAD_SIZE
    context_group = queries.shape[1] // keys.shape[1]

    slots, chosen, pass_last = gather_window(jnp.stack([keys, values]), n, window)
    half = window // 2
    first = [pairs[:-2] for pairs in chosen]
    last = [pairs[-2:] for pairs in chosen]

    prompt_ids = jnp.arange(group_widths.shape[0], dtype=jnp.int32)
    offsets = jnp.sum(
        jnp.where(prompt_ids[None, :] < prompt_ids[:, None], group_widths[None, :], 0), axis=1
    )
    owner = jnp.sum((offsets <= group_index).astype(jnp.int32)) - 1
    picked = prompt_ids == owner
    start = jnp.sum(jnp.where(picked, offsets, 0))
    width = jnp.sum(jnp.where(picked, group_widths, 0))
    padding = jnp.sum(jnp.where(picked, pad_tokens, 0))
    length = width * rows_here - padding
    local_rows = jnp.arange(rows_here, dtype=jnp.int32)
    query_pos = (group_index - start) * rows_here + local_rows

    def key_position(shift):
        return (((group_index - shift - start) * rows_here)[:, None] + local_rows[None, :]).reshape(-1)

    place = (query_pos, key_position, length, group_index % 2)
    zero = jnp.int32(0)
    carry = attend_stage(place, queries, slots, first, heads_kv, peer=zero)
    newest, carry = lax.optimization_barrier((slots[half], carry))
    slots = slots[:half] + [newest] + slots[half + 1:] + [pass_last(newest)]

    n_tp = lax.axis_size("tp")
    if n_tp == 2:
        me = lax.axis_index("tp")
        attended, peer_terms = attend_stage(
            place, queries, slots, last, heads_kv, carry=carry, out_weight=out_weight, peer=1 - me
        )
        got = lax.ppermute(peer_terms, "tp", [(0, 1), (1, 0)])
        part = out_weight.shape[1] // 2
        own_weight = lax.dynamic_slice_in_dim(out_weight, me * part, part, 1)
        own_terms = jnp.dot(attended, own_weight, preferred_element_type=jnp.float32)
        own_terms = lax.optimization_barrier(own_terms.astype(jnp.bfloat16)).astype(jnp.float32)
        return (own_terms + got.astype(jnp.float32)).astype(jnp.bfloat16)
    (attended,) = attend_stage(place, queries, slots, last, heads_kv, carry=carry, peer=zero)
    terms = jnp.dot(attended, out_weight, preferred_element_type=jnp.float32)
    return lax.psum_scatter(terms.astype(jnp.bfloat16), "tp", scatter_dimension=1, tiled=True)


def solution(mesh):
    return jax.shard_map(
        on_device,
        mesh=mesh,
        in_specs=(P("ctx", "tp"), P("ctx", "tp"), P("ctx", "tp"), P("tp", None), P(), P()),
        out_specs=P("ctx", "tp"),
        check_vma=False,
    )
```

```python
import functools
import math

import jax
import jax.numpy as jnp
from jax import lax
from jax.experimental import pallas as pl
from jax.experimental.pallas import tpu as pltpu
from jax.sharding import PartitionSpec as P

HEAD_SIZE = 128
FAR = 1 << 20


def gather_window(kv, n, window):
    half = window // 2
    received = [None] * half
    for m in reversed(range(half)):
        s = 2 * m + 1
        if s == 1:
            pairs = [(j, j + 1) for j in range(1, n - 1, 2)]
        else:
            pairs = [(j, j + s) for j in range(n - s)]
        received[m] = lax.ppermute(kv, "ctx", pairs)
    up = [(j, j + 1) for j in range(0, n, 2)]
    down = [(j + 1, j) for j in range(0, n, 2)]
    passed = [lax.ppermute(kv, "ctx", up)]
    for m in range(half):
        pairs = (up if m < half - 1 else []) + (down if m > 0 else [])
        passed.append(lax.ppermute(received[m], "ctx", pairs))
    slots = [kv] + received + passed
    even_use = [0] + [1 + m for m in range(half)] + [2 + half + m for m in range(1, half)]
    odd_use = [0] + [1 + m for m in range(1, half)] + [1 + half] + [2 + half + m for m in range(half - 1)]
    even_shift = [0] + [2 * m + 1 for m in range(half)] + [2 * m for m in range(1, half)]
    odd_shift = [0] + [2 * m + 1 for m in range(1, half)] + [1] + [2 * m + 2 for m in range(half - 1)]
    core = lax.axis_index("ctx") % 2
    shift = jnp.where(core == 0, jnp.array(even_shift, jnp.int32), jnp.array(odd_shift, jnp.int32))
    return slots, (even_use, odd_use), shift


def turn(rows, cosine, sine):
    rows = rows.astype(jnp.float32)
    return (rows * cosine + pltpu.roll(rows, HEAD_SIZE // 2, 1) * sine).astype(jnp.bfloat16)


def attention_kernel(n_slots, uses, heads_kv, project, peer_ref, core_ref, query_pos_ref, key_limit_ref,
                     query_cos_ref, query_sin_ref, key_cos_ref, key_sin_ref, query_ref, *refs):
    slot_refs = refs[:n_slots]
    if project:
        weight_hbm, out_ref, peer_out_ref, weight_ref, copy_sem = refs[n_slots:]
        group = query_ref.shape[1] // heads_kv
        part = weight_ref.shape[1]
        copies = [
            pltpu.make_async_copy(
                weight_hbm.at[pl.ds(h * group, group), pl.ds(pl.multiple_of(peer_ref[0] * part, part), part)],
                weight_ref.at[pl.ds(h * group, group), :],
                copy_sem.at[h],
            )
            for h in range(heads_kv)
        ]
        for copy in copies:
            copy.start()
    else:
        (out_ref,) = refs[n_slots:]
    allowed = key_limit_ref[...] <= query_pos_ref[...]
    heads_here = query_ref.shape[1] // HEAD_SIZE // heads_kv

    def body(use):
        for h in range(heads_kv):
            head = slice(h * HEAD_SIZE, (h + 1) * HEAD_SIZE)
            keys = turn(jnp.concatenate([slot_refs[j][0, :, head] for j in use], axis=0),
                        key_cos_ref[...], key_sin_ref[...])
            values = jnp.concatenate([slot_refs[j][1, :, head] for j in use], axis=0)
            for g in range(heads_here):
                q = h * heads_here + g
                columns = slice(q * HEAD_SIZE, (q + 1) * HEAD_SIZE)
                query = turn(query_ref[:, columns], query_cos_ref[...], query_sin_ref[...])
                scores = lax.dot_general(
                    query, keys, (((1,), (1,)), ((), ())), preferred_element_type=jnp.float32
                ) * (1.0 / math.sqrt(HEAD_SIZE))
                scores = jnp.where(allowed, scores, -1e30)
                highest = jnp.max(scores, axis=1, keepdims=True)
                weights = jnp.exp(scores - highest)
                totals = jnp.sum(weights, axis=1, keepdims=True)
                summed = jnp.dot(weights.astype(jnp.bfloat16), values, preferred_element_type=jnp.float32)
                out_ref[:, columns] = (summed / totals).astype(out_ref.dtype)

    for parity, use in enumerate(uses):
        pl.when(core_ref[0] == parity)(functools.partial(body, use))
    if project:
        total = None
        for h in range(heads_kv):
            copies[h].wait()
            rows = slice(h * group, (h + 1) * group)
            term = jnp.dot(out_ref[:, rows], weight_ref[rows, :], preferred_element_type=jnp.float32)
            total = term if total is None else total + term
        peer_out_ref[...] = total.astype(peer_out_ref.dtype)


def tables(positions):
    half = HEAD_SIZE // 2
    freqs = 500000.0 ** (-jnp.arange(half, dtype=jnp.float32) / half)
    angles = positions.astype(jnp.float32)[:, None] * freqs[None, :]
    cosine = jnp.cos(angles)
    sine = jnp.sin(angles)
    return jnp.concatenate([cosine, cosine], axis=1), jnp.concatenate([-sine, sine], axis=1)


def attend(query_pos, key_pos, key_limit, queries, slots, uses, heads_kv, out_weight, peer):
    rows, width = queries.shape
    n_slots = len(slots)
    count = key_pos.shape[0]
    project = out_weight is not None
    query_cos, query_sin = tables(query_pos)
    key_cos, key_sin = tables(key_pos)
    vmem = pl.BlockSpec(memory_space=pltpu.VMEM)
    smem = pl.BlockSpec(memory_space=pltpu.SMEM)
    core = (lax.axis_index("ctx") % 2).astype(jnp.int32)
    args = [peer.reshape(1), core.reshape(1), query_pos.reshape(rows, 1), key_limit, query_cos, query_sin,
            key_cos, key_sin, queries] + slots
    in_specs = [smem, smem] + [vmem] * (7 + n_slots)
    out_shape = [jax.ShapeDtypeStruct((rows, width), jnp.bfloat16)]
    out_specs = [vmem]
    scratch = []
    flops = 4 * rows * count * width
    moved = 2 * (2 * rows * width + 2 * count * heads_kv * HEAD_SIZE)
    if project:
        part = out_weight.shape[1] // 2
        args.append(out_weight)
        in_specs.append(pl.BlockSpec(memory_space=pl.ANY))
        out_shape.append(jax.ShapeDtypeStruct((rows, part), jnp.bfloat16))
        out_specs.append(vmem)
        scratch += [pltpu.VMEM((width, part), jnp.bfloat16), pltpu.SemaphoreType.DMA((heads_kv,))]
        flops += 2 * rows * width * part
        moved += 2 * (width * part + rows * part)
    return pl.pallas_call(
        functools.partial(attention_kernel, n_slots, uses, heads_kv, project),
        out_shape=out_shape,
        in_specs=in_specs,
        out_specs=out_specs,
        scratch_shapes=scratch,
        compiler_params=pltpu.CompilerParams(vmem_limit_bytes=48 * 1024 * 1024),
        cost_estimate=pl.CostEstimate(
            flops=flops, transcendentals=rows * count * width // HEAD_SIZE, bytes_accessed=moved
        ),
    )(*args)


def on_device(queries, keys, values, out_weight, group_widths, pad_tokens):
    n = lax.axis_size("ctx")
    window = n // 2
    group_index = lax.axis_index("ctx")
    rows_here = queries.shape[0]
    heads_kv = keys.shape[1] // HEAD_SIZE
    context_group = queries.shape[1] // keys.shape[1]

    slots, uses, shift = gather_window(jnp.stack([keys, values]), n, window)

    prompt_ids = jnp.arange(group_widths.shape[0], dtype=jnp.int32)
    offsets = jnp.sum(
        jnp.where(prompt_ids[None, :] < prompt_ids[:, None], group_widths[None, :], 0), axis=1
    )
    owner = jnp.sum((offsets <= group_index).astype(jnp.int32)) - 1
    picked = prompt_ids == owner
    start = jnp.sum(jnp.where(picked, offsets, 0))
    width = jnp.sum(jnp.where(picked, group_widths, 0))
    padding = jnp.sum(jnp.where(picked, pad_tokens, 0))
    length = width * rows_here - padding
    local_rows = jnp.arange(rows_here, dtype=jnp.int32)
    query_pos = (group_index - start) * rows_here + local_rows
    key_pos = ((group_index - shift - start) * rows_here)[:, None] + local_rows[None, :]
    key_pos = key_pos.reshape(-1)

    usable = (key_pos >= 0) & (key_pos < length)
    key_limit = jnp.where(usable, key_pos, FAR * rows_here).reshape(1, -1)

    n_tp = lax.axis_size("tp")
    if n_tp == 2:
        me = lax.axis_index("tp")
        attended, peer_terms = attend(
            query_pos, key_pos, key_limit, queries, slots, uses, heads_kv, out_weight, 1 - me
        )
        got = lax.ppermute(peer_terms, "tp", [(0, 1), (1, 0)])
        part = out_weight.shape[1] // 2
        own_weight = lax.dynamic_slice_in_dim(out_weight, me * part, part, 1)
        own_terms = jnp.dot(attended, own_weight, preferred_element_type=jnp.float32)
        own_terms = lax.optimization_barrier(own_terms.astype(jnp.bfloat16)).astype(jnp.float32)
        return (own_terms + got.astype(jnp.float32)).astype(jnp.bfloat16)
    (attended,) = attend(query_pos, key_pos, key_limit, queries, slots, uses, heads_kv, None, jnp.int32(0))
    terms = jnp.dot(attended, out_weight, preferred_element_type=jnp.float32)
    return lax.psum_scatter(terms.astype(jnp.bfloat16), "tp", scatter_dimension=1, tiled=True)


def solution(mesh):
    return jax.shard_map(
        on_device,
        mesh=mesh,
        in_specs=(P("ctx", "tp"), P("ctx", "tp"), P("ctx", "tp"), P("tp", None), P(), P()),
        out_specs=P("ctx", "tp"),
        check_vma=False,
    )
```

```python
import functools
import math

import jax
import jax.numpy as jnp
from jax import lax
from jax.experimental import pallas as pl
from jax.experimental.pallas import tpu as pltpu
from jax.sharding import PartitionSpec as P

HEAD_SIZE = 128
FAR = 1 << 20


def gather_window(kv, n, window):
    half = window // 2
    received = [None] * half
    for m in reversed(range(half)):
        s = 2 * m + 1
        if s == 1:
            pairs = [(j, j + 1) for j in range(1, n - 1, 2)]
        else:
            pairs = [(j, j + s) for j in range(n - s)]
        received[m] = lax.ppermute(kv, "ctx", pairs)
        if m == half - 1:
            direct = lax.ppermute(kv, "ctx", [(j, j + s - 1) for j in range(0, n - s + 1, 2)])
    up = [(j, j + 1) for j in range(0, n, 2)]
    down = [(j + 1, j) for j in range(0, n, 2)]
    passed = [lax.ppermute(kv, "ctx", up)]
    for m in range(half - 1):
        passed.append(lax.ppermute(received[m], "ctx", up + (down if m > 0 else [])))
    slots = [kv] + received + [direct] + passed
    even = [(0, 0)] + [(1 + m, 2 * m + 1) for m in range(half)]
    even += [(3 + half + m, 2 * m) for m in range(1, half - 1)] + [(1 + half, window - 2)]
    odd = [(0, 0)] + [(1 + m, 2 * m + 1) for m in range(1, half)] + [(2 + half, 1)]
    odd += [(3 + half + m, 2 * m + 2) for m in range(half - 1)]
    core = lax.axis_index("ctx") % 2
    shift = jnp.where(core == 0, jnp.array([t for _, t in even], jnp.int32),
                      jnp.array([t for _, t in odd], jnp.int32))
    return slots, ([s for s, _ in even], [s for s, _ in odd]), shift


def turn(rows, cosine, sine):
    rows = rows.astype(jnp.float32)
    return (rows * cosine + pltpu.roll(rows, HEAD_SIZE // 2, 1) * sine).astype(jnp.bfloat16)


def attention_kernel(n_slots, uses, heads_kv, project, peer_ref, core_ref, query_pos_ref, key_limit_ref,
                     query_cos_ref, query_sin_ref, key_cos_ref, key_sin_ref, query_any, *refs):
    slot_any = refs[:n_slots]
    refs = refs[n_slots:]
    if project:
        weight_hbm, out_ref, peer_out_ref, query_ref, slot_ref, load_sem, weight_ref, copy_sem = refs
        group = query_ref.shape[1] // heads_kv
        part = weight_ref.shape[1]
        copies = [
            pltpu.make_async_copy(
                weight_hbm.at[pl.ds(h * group, group), pl.ds(pl.multiple_of(peer_ref[0] * part, part), part)],
                weight_ref.at[pl.ds(h * group, group), :],
                copy_sem.at[h],
            )
            for h in range(heads_kv)
        ]
        for copy in copies:
            copy.start()
    else:
        out_ref, query_ref, slot_ref, load_sem = refs
    loads = [pltpu.make_async_copy(query_any, query_ref, load_sem.at[n_slots])]
    loads += [pltpu.make_async_copy(slot_any[j], slot_ref.at[j], load_sem.at[j]) for j in range(n_slots)]
    for load in loads:
        load.start()
    for load in loads:
        load.wait()
    allowed = key_limit_ref[...] <= query_pos_ref[...]
    heads_here = query_ref.shape[1] // HEAD_SIZE // heads_kv

    def body(use):
        for h in range(heads_kv):
            head = slice(h * HEAD_SIZE, (h + 1) * HEAD_SIZE)
            keys = turn(jnp.concatenate([slot_ref[j, 0, :, head] for j in use], axis=0),
                        key_cos_ref[...], key_sin_ref[...])
            values = jnp.concatenate([slot_ref[j, 1, :, head] for j in use], axis=0)
            for g in range(heads_here):
                q = h * heads_here + g
                columns = slice(q * HEAD_SIZE, (q + 1) * HEAD_SIZE)
                query = turn(query_ref[:, columns], query_cos_ref[...], query_sin_ref[...])
                scores = lax.dot_general(
                    query, keys, (((1,), (1,)), ((), ())), preferred_element_type=jnp.float32
                ) * (1.0 / math.sqrt(HEAD_SIZE))
                scores = jnp.where(allowed, scores, -1e30)
                highest = jnp.max(scores, axis=1, keepdims=True)
                weights = jnp.exp(scores - highest)
                totals = jnp.sum(weights, axis=1, keepdims=True)
                summed = jnp.dot(weights.astype(jnp.bfloat16), values, preferred_element_type=jnp.float32)
                out_ref[:, columns] = (summed / totals).astype(out_ref.dtype)

    for parity, use in enumerate(uses):
        pl.when(core_ref[0] == parity)(functools.partial(body, use))
    if project:
        total = None
        for h in range(heads_kv):
            copies[h].wait()
            rows = slice(h * group, (h + 1) * group)
            term = jnp.dot(out_ref[:, rows], weight_ref[rows, :], preferred_element_type=jnp.float32)
            total = term if total is None else total + term
        peer_out_ref[...] = total.astype(peer_out_ref.dtype)


def tables(positions):
    half = HEAD_SIZE // 2
    freqs = 500000.0 ** (-jnp.arange(half, dtype=jnp.float32) / half)
    angles = positions.astype(jnp.float32)[:, None] * freqs[None, :]
    cosine = jnp.cos(angles)
    sine = jnp.sin(angles)
    return jnp.concatenate([cosine, cosine], axis=1), jnp.concatenate([-sine, sine], axis=1)


def attend(query_pos, key_pos, key_limit, queries, slots, uses, heads_kv, out_weight, peer):
    rows, width = queries.shape
    n_slots = len(slots)
    count = key_pos.shape[0]
    project = out_weight is not None
    query_cos, query_sin = tables(query_pos)
    key_cos, key_sin = tables(key_pos)
    smem = pl.BlockSpec(memory_space=pltpu.SMEM)

    def vmem(shape):
        return pl.BlockSpec(shape, lambda: (0,) * len(shape))

    core = (lax.axis_index("ctx") % 2).astype(jnp.int32)
    args = [peer.reshape(1), core.reshape(1), query_pos.reshape(rows, 1), key_limit, query_cos, query_sin,
            key_cos, key_sin, queries] + slots
    anywhere = pl.BlockSpec(memory_space=pl.ANY)
    in_specs = [smem, smem] + [vmem(x.shape) for x in args[2:8]] + [anywhere] * (1 + n_slots)
    out_shape = [jax.ShapeDtypeStruct((rows, width), jnp.bfloat16)]
    out_specs = [vmem((rows, width))]
    scratch = [pltpu.VMEM((rows, width), jnp.bfloat16), pltpu.VMEM((n_slots,) + slots[0].shape, jnp.bfloat16),
               pltpu.SemaphoreType.DMA((n_slots + 1,))]
    flops = 4 * rows * count * width
    moved = 2 * (2 * rows * width + 2 * count * heads_kv * HEAD_SIZE)
    if project:
        part = out_weight.shape[1] // 2
        args.append(out_weight)
        in_specs.append(anywhere)
        out_shape.append(jax.ShapeDtypeStruct((rows, part), jnp.bfloat16))
        out_specs.append(vmem((rows, part)))
        scratch += [pltpu.VMEM((width, part), jnp.bfloat16), pltpu.SemaphoreType.DMA((heads_kv,))]
        flops += 2 * rows * width * part
        moved += 2 * (width * part + rows * part)
    return pl.pallas_call(
        functools.partial(attention_kernel, n_slots, uses, heads_kv, project),
        out_shape=out_shape,
        in_specs=in_specs,
        out_specs=out_specs,
        scratch_shapes=scratch,
        compiler_params=pltpu.CompilerParams(vmem_limit_bytes=48 * 1024 * 1024),
        cost_estimate=pl.CostEstimate(
            flops=flops, transcendentals=rows * count * width // HEAD_SIZE, bytes_accessed=moved
        ),
    )(*args)


def on_device(queries, keys, values, out_weight, group_widths, pad_tokens):
    n = lax.axis_size("ctx")
    window = n // 2
    group_index = lax.axis_index("ctx")
    rows_here = queries.shape[0]
    heads_kv = keys.shape[1] // HEAD_SIZE
    context_group = queries.shape[1] // keys.shape[1]

    slots, uses, shift = gather_window(jnp.stack([keys, values]), n, window)

    prompt_ids = jnp.arange(group_widths.shape[0], dtype=jnp.int32)
    offsets = jnp.sum(
        jnp.where(prompt_ids[None, :] < prompt_ids[:, None], group_widths[None, :], 0), axis=1
    )
    owner = jnp.sum((offsets <= group_index).astype(jnp.int32)) - 1
    picked = prompt_ids == owner
    start = jnp.sum(jnp.where(picked, offsets, 0))
    width = jnp.sum(jnp.where(picked, group_widths, 0))
    padding = jnp.sum(jnp.where(picked, pad_tokens, 0))
    length = width * rows_here - padding
    local_rows = jnp.arange(rows_here, dtype=jnp.int32)
    query_pos = (group_index - start) * rows_here + local_rows
    key_pos = ((group_index - shift - start) * rows_here)[:, None] + local_rows[None, :]
    key_pos = key_pos.reshape(-1)

    usable = (key_pos >= 0) & (key_pos < length)
    key_limit = jnp.where(usable, key_pos, FAR * rows_here).reshape(1, -1)

    n_tp = lax.axis_size("tp")
    if n_tp == 2:
        me = lax.axis_index("tp")
        attended, peer_terms = attend(
            query_pos, key_pos, key_limit, queries, slots, uses, heads_kv, out_weight, 1 - me
        )
        got = lax.ppermute(peer_terms, "tp", [(0, 1), (1, 0)])
        part = out_weight.shape[1] // 2
        own_weight = lax.dynamic_slice_in_dim(out_weight, me * part, part, 1)
        own_terms = jnp.dot(attended, own_weight, preferred_element_type=jnp.float32)
        own_terms = lax.optimization_barrier(own_terms.astype(jnp.bfloat16)).astype(jnp.float32)
        return (own_terms + got.astype(jnp.float32)).astype(jnp.bfloat16)
    (attended,) = attend(query_pos, key_pos, key_limit, queries, slots, uses, heads_kv, None, jnp.int32(0))
    terms = jnp.dot(attended, out_weight, preferred_element_type=jnp.float32)
    return lax.psum_scatter(terms.astype(jnp.bfloat16), "tp", scatter_dimension=1, tiled=True)


def solution(mesh):
    return jax.shard_map(
        on_device,
        mesh=mesh,
        in_specs=(P("ctx", "tp"), P("ctx", "tp"), P("ctx", "tp"), P("tp", None), P(), P()),
        out_specs=P("ctx", "tp"),
        check_vma=False,
    )
```

```python
import functools
import math

import jax
import jax.numpy as jnp
from jax import lax
from jax.experimental import pallas as pl
from jax.experimental.pallas import tpu as pltpu
from jax.sharding import PartitionSpec as P

HEAD_SIZE = 128
FAR = 1 << 20


def gather_window(kv, n, window):
    received = []
    for s in range(1, window, 2):
        if s == 1:
            pairs = [(j, j + 1) for j in range(1, n - 1, 2)]
        else:
            pairs = [(j, j + s) for j in range(n - s)]
        received.append(lax.ppermute(kv, "ctx", pairs))
    across = [(j, j ^ 1) for j in range(n)]
    passed = [lax.ppermute(block, "ctx", across) for block in [kv] + received]
    half = window // 2
    even_shift = [0] + [2 * m + 1 for m in range(half)] + [FAR, FAR] + [2 * m for m in range(1, half)]
    odd_shift = [0, FAR] + [2 * m + 1 for m in range(1, half)] + [1] + [2 * m + 2 for m in range(half)]
    core = lax.axis_index("ctx") % 2
    shift = jnp.where(core == 0, jnp.array(even_shift, jnp.int32), jnp.array(odd_shift, jnp.int32))
    return [kv] + received + passed, shift


def turn(rows, cosine, sine):
    rows = rows.astype(jnp.float32)
    return (rows * cosine + pltpu.roll(rows, HEAD_SIZE // 2, 1) * sine).astype(jnp.bfloat16)


def attention_kernel(n_slots, uses, heads_kv, project, peer_ref, core_ref, query_pos_ref, key_limit_ref,
                     query_cos_ref, query_sin_ref, key_cos_ref, key_sin_ref, query_ref, *refs):
    slot_refs = refs[:n_slots]
    if project:
        weight_hbm, out_ref, peer_out_ref, weight_ref, copy_sem = refs[n_slots:]
        group = query_ref.shape[1] // heads_kv
        part = weight_ref.shape[1]
        copies = [
            pltpu.make_async_copy(
                weight_hbm.at[pl.ds(h * group, group), pl.ds(pl.multiple_of(peer_ref[0] * part, part), part)],
                weight_ref.at[pl.ds(h * group, group), :],
                copy_sem.at[h],
            )
            for h in range(heads_kv)
        ]
        for copy in copies:
            copy.start()
    else:
        (out_ref,) = refs[n_slots:]
    allowed = key_limit_ref[...] <= query_pos_ref[...]
    heads_here = query_ref.shape[1] // HEAD_SIZE // heads_kv

    def body(use):
        for h in range(heads_kv):
            head = slice(h * HEAD_SIZE, (h + 1) * HEAD_SIZE)
            keys = turn(jnp.concatenate([slot_refs[j][0, :, head] for j in use], axis=0),
                        key_cos_ref[...], key_sin_ref[...])
            values = jnp.concatenate([slot_refs[j][1, :, head] for j in use], axis=0)
            for g in range(heads_here):
                q = h * heads_here + g
                columns = slice(q * HEAD_SIZE, (q + 1) * HEAD_SIZE)
                query = turn(query_ref[:, columns], query_cos_ref[...], query_sin_ref[...])
                scores = lax.dot_general(
                    query, keys, (((1,), (1,)), ((), ())), preferred_element_type=jnp.float32
                ) * (1.0 / math.sqrt(HEAD_SIZE))
                scores = jnp.where(allowed, scores, -1e30)
                highest = jnp.max(scores, axis=1, keepdims=True)
                weights = jnp.exp(scores - highest)
                totals = jnp.sum(weights, axis=1, keepdims=True)
                summed = jnp.dot(weights.astype(jnp.bfloat16), values, preferred_element_type=jnp.float32)
                out_ref[:, columns] = (summed / totals).astype(out_ref.dtype)

    body(uses)
    if project:
        total = None
        for h in range(heads_kv):
            copies[h].wait()
            rows = slice(h * group, (h + 1) * group)
            term = jnp.dot(out_ref[:, rows], weight_ref[rows, :], preferred_element_type=jnp.float32)
            total = term if total is None else total + term
        peer_out_ref[...] = total.astype(peer_out_ref.dtype)


def tables(positions):
    half = HEAD_SIZE // 2
    freqs = 500000.0 ** (-jnp.arange(half, dtype=jnp.float32) / half)
    angles = positions.astype(jnp.float32)[:, None] * freqs[None, :]
    cosine = jnp.cos(angles)
    sine = jnp.sin(angles)
    return jnp.concatenate([cosine, cosine], axis=1), jnp.concatenate([-sine, sine], axis=1)


def attend(query_pos, key_pos, key_limit, queries, slots, uses, heads_kv, out_weight, peer):
    rows, width = queries.shape
    n_slots = len(slots)
    count = key_pos.shape[0]
    project = out_weight is not None
    query_cos, query_sin = tables(query_pos)
    key_cos, key_sin = tables(key_pos)
    vmem = pl.BlockSpec(memory_space=pltpu.VMEM)
    smem = pl.BlockSpec(memory_space=pltpu.SMEM)
    core = (lax.axis_index("ctx") % 2).astype(jnp.int32)
    args = [peer.reshape(1), core.reshape(1), query_pos.reshape(rows, 1), key_limit, query_cos, query_sin,
            key_cos, key_sin, queries] + slots
    in_specs = [smem, smem] + [vmem] * (7 + n_slots)
    out_shape = [jax.ShapeDtypeStruct((rows, width), jnp.bfloat16)]
    out_specs = [vmem]
    scratch = []
    flops = 4 * rows * count * width
    moved = 2 * (2 * rows * width + 2 * count * heads_kv * HEAD_SIZE)
    if project:
        part = out_weight.shape[1] // 2
        args.append(out_weight)
        in_specs.append(pl.BlockSpec(memory_space=pl.ANY))
        out_shape.append(jax.ShapeDtypeStruct((rows, part), jnp.bfloat16))
        out_specs.append(vmem)
        scratch += [pltpu.VMEM((width, part), jnp.bfloat16), pltpu.SemaphoreType.DMA((heads_kv,))]
        flops += 2 * rows * width * part
        moved += 2 * (width * part + rows * part)
    return pl.pallas_call(
        functools.partial(attention_kernel, n_slots, uses, heads_kv, project),
        out_shape=out_shape,
        in_specs=in_specs,
        out_specs=out_specs,
        scratch_shapes=scratch,
        compiler_params=pltpu.CompilerParams(vmem_limit_bytes=48 * 1024 * 1024),
        cost_estimate=pl.CostEstimate(
            flops=flops, transcendentals=rows * count * width // HEAD_SIZE, bytes_accessed=moved
        ),
    )(*args)


def on_device(queries, keys, values, out_weight, group_widths, pad_tokens):
    n = lax.axis_size("ctx")
    window = n // 2
    group_index = lax.axis_index("ctx")
    rows_here = queries.shape[0]
    heads_kv = keys.shape[1] // HEAD_SIZE
    context_group = queries.shape[1] // keys.shape[1]

    slots, shift = gather_window(jnp.stack([keys, values]), n, window)

    prompt_ids = jnp.arange(group_widths.shape[0], dtype=jnp.int32)
    offsets = jnp.sum(
        jnp.where(prompt_ids[None, :] < prompt_ids[:, None], group_widths[None, :], 0), axis=1
    )
    owner = jnp.sum((offsets <= group_index).astype(jnp.int32)) - 1
    picked = prompt_ids == owner
    start = jnp.sum(jnp.where(picked, offsets, 0))
    width = jnp.sum(jnp.where(picked, group_widths, 0))
    padding = jnp.sum(jnp.where(picked, pad_tokens, 0))
    length = width * rows_here - padding
    local_rows = jnp.arange(rows_here, dtype=jnp.int32)
    query_pos = (group_index - start) * rows_here + local_rows
    key_pos = ((group_index - shift - start) * rows_here)[:, None] + local_rows[None, :]
    key_pos = key_pos.reshape(-1)

    usable = (key_pos >= 0) & (key_pos < length)
    key_limit = jnp.where(usable, key_pos, FAR * rows_here).reshape(1, -1)

    n_tp = lax.axis_size("tp")
    if n_tp == 2:
        me = lax.axis_index("tp")
        attended, peer_terms = attend(
            query_pos, key_pos, key_limit, queries, slots, list(range(len(slots))), heads_kv, out_weight, 1 - me
        )
        got = lax.ppermute(peer_terms, "tp", [(0, 1), (1, 0)])
        part = out_weight.shape[1] // 2
        own_weight = lax.dynamic_slice_in_dim(out_weight, me * part, part, 1)
        own_terms = jnp.dot(attended, own_weight, preferred_element_type=jnp.float32)
        own_terms = lax.optimization_barrier(own_terms.astype(jnp.bfloat16)).astype(jnp.float32)
        return (own_terms + got.astype(jnp.float32)).astype(jnp.bfloat16)
    (attended,) = attend(query_pos, key_pos, key_limit, queries, slots, list(range(len(slots))), heads_kv, None, jnp.int32(0))
    terms = jnp.dot(attended, out_weight, preferred_element_type=jnp.float32)
    return lax.psum_scatter(terms.astype(jnp.bfloat16), "tp", scatter_dimension=1, tiled=True)


def solution(mesh):
    return jax.shard_map(
        on_device,
        mesh=mesh,
        in_specs=(P("ctx", "tp"), P("ctx", "tp"), P("ctx", "tp"), P("tp", None), P(), P()),
        out_specs=P("ctx", "tp"),
        check_vma=False,
    )
```

```python
import functools
import math

import jax
import jax.numpy as jnp
from jax import lax
from jax.experimental import pallas as pl
from jax.experimental.pallas import tpu as pltpu
from jax.sharding import PartitionSpec as P

HEAD_SIZE = 128
FAR = 1 << 20


def gather_window(kv, n, window):
    received = []
    for s in range(1, window, 2):
        if s == 1:
            pairs = [(j, j + 1) for j in range(1, n - 1, 2)]
        else:
            pairs = [(j, j + s) for j in range(n - s)]
        received.append(lax.ppermute(kv, "ctx", pairs))
    across = [(j, j ^ 1) for j in range(n)]
    passed = [lax.ppermute(block, "ctx", across) for block in [kv] + received]
    half = window // 2
    even = [(0, 0)] + [(1 + m, 2 * m + 1) for m in range(half)] + [(2 + half + m, 2 * m) for m in range(1, half)]
    odd = [(0, 0)] + [(1 + m, 2 * m + 1) for m in range(1, half)] + [(1 + half, 1)]
    odd += [(2 + half + m, 2 * m + 2) for m in range(half - 1)]
    core = lax.axis_index("ctx") % 2
    shift = jnp.where(core == 0, jnp.array([t for _, t in even], jnp.int32),
                      jnp.array([t for _, t in odd], jnp.int32))
    return [kv] + received + passed, ([s for s, _ in even], [s for s, _ in odd]), shift


def turn(rows, cosine, sine):
    rows = rows.astype(jnp.float32)
    return (rows * cosine + pltpu.roll(rows, HEAD_SIZE // 2, 1) * sine).astype(jnp.bfloat16)


def attention_kernel(n_slots, uses, heads_kv, project, peer_ref, core_ref, query_pos_ref, key_limit_ref,
                     query_cos_ref, query_sin_ref, key_cos_ref, key_sin_ref, query_ref, *refs):
    slot_refs = refs[:n_slots]
    if project:
        weight_hbm, out_ref, peer_out_ref, weight_ref, copy_sem = refs[n_slots:]
        group = query_ref.shape[1] // heads_kv
        part = weight_ref.shape[1]
        copies = [
            pltpu.make_async_copy(
                weight_hbm.at[pl.ds(h * group, group), pl.ds(pl.multiple_of(peer_ref[0] * part, part), part)],
                weight_ref.at[pl.ds(h * group, group), :],
                copy_sem.at[h],
            )
            for h in range(heads_kv)
        ]
        for copy in copies:
            copy.start()
    else:
        (out_ref,) = refs[n_slots:]
    allowed = key_limit_ref[...] <= query_pos_ref[...]
    heads_here = query_ref.shape[1] // HEAD_SIZE // heads_kv

    def body(use):
        for h in range(heads_kv):
            head = slice(h * HEAD_SIZE, (h + 1) * HEAD_SIZE)
            keys = turn(jnp.concatenate([slot_refs[j][0, :, head] for j in use], axis=0),
                        key_cos_ref[...], key_sin_ref[...])
            values = jnp.concatenate([slot_refs[j][1, :, head] for j in use], axis=0)
            for g in range(heads_here):
                q = h * heads_here + g
                columns = slice(q * HEAD_SIZE, (q + 1) * HEAD_SIZE)
                query = turn(query_ref[:, columns], query_cos_ref[...], query_sin_ref[...])
                scores = lax.dot_general(
                    query, keys, (((1,), (1,)), ((), ())), preferred_element_type=jnp.float32
                ) * (1.0 / math.sqrt(HEAD_SIZE))
                scores = jnp.where(allowed, scores, -1e30)
                highest = jnp.max(scores, axis=1, keepdims=True)
                weights = jnp.exp(scores - highest)
                totals = jnp.sum(weights, axis=1, keepdims=True)
                summed = jnp.dot(weights.astype(jnp.bfloat16), values, preferred_element_type=jnp.float32)
                out_ref[:, columns] = (summed / totals).astype(out_ref.dtype)

    for parity, use in enumerate(uses):
        pl.when(core_ref[0] == parity)(functools.partial(body, use))
    if project:
        total = None
        for h in range(heads_kv):
            copies[h].wait()
            rows = slice(h * group, (h + 1) * group)
            term = jnp.dot(out_ref[:, rows], weight_ref[rows, :], preferred_element_type=jnp.float32)
            total = term if total is None else total + term
        peer_out_ref[...] = total.astype(peer_out_ref.dtype)


def tables(positions):
    half = HEAD_SIZE // 2
    freqs = 500000.0 ** (-jnp.arange(half, dtype=jnp.float32) / half)
    angles = positions.astype(jnp.float32)[:, None] * freqs[None, :]
    cosine = jnp.cos(angles)
    sine = jnp.sin(angles)
    return jnp.concatenate([cosine, cosine], axis=1), jnp.concatenate([-sine, sine], axis=1)


def attend(query_pos, key_pos, key_limit, queries, slots, uses, heads_kv, out_weight, peer):
    rows, width = queries.shape
    n_slots = len(slots)
    count = key_pos.shape[0]
    project = out_weight is not None
    query_cos, query_sin = tables(query_pos)
    key_cos, key_sin = tables(key_pos)
    vmem = pl.BlockSpec(memory_space=pltpu.VMEM)
    smem = pl.BlockSpec(memory_space=pltpu.SMEM)
    core = (lax.axis_index("ctx") % 2).astype(jnp.int32)
    args = [peer.reshape(1), core.reshape(1), query_pos.reshape(rows, 1), key_limit, query_cos, query_sin,
            key_cos, key_sin, queries] + slots
    in_specs = [smem, smem] + [vmem] * (7 + n_slots)
    out_shape = [jax.ShapeDtypeStruct((rows, width), jnp.bfloat16)]
    out_specs = [vmem]
    scratch = []
    flops = 4 * rows * count * width
    moved = 2 * (2 * rows * width + 2 * count * heads_kv * HEAD_SIZE)
    if project:
        part = out_weight.shape[1] // 2
        args.append(out_weight)
        in_specs.append(pl.BlockSpec(memory_space=pl.ANY))
        out_shape.append(jax.ShapeDtypeStruct((rows, part), jnp.bfloat16))
        out_specs.append(vmem)
        scratch += [pltpu.VMEM((width, part), jnp.bfloat16), pltpu.SemaphoreType.DMA((heads_kv,))]
        flops += 2 * rows * width * part
        moved += 2 * (width * part + rows * part)
    return pl.pallas_call(
        functools.partial(attention_kernel, n_slots, uses, heads_kv, project),
        out_shape=out_shape,
        in_specs=in_specs,
        out_specs=out_specs,
        scratch_shapes=scratch,
        compiler_params=pltpu.CompilerParams(vmem_limit_bytes=48 * 1024 * 1024),
        cost_estimate=pl.CostEstimate(
            flops=flops, transcendentals=rows * count * width // HEAD_SIZE, bytes_accessed=moved
        ),
    )(*args)


def on_device(queries, keys, values, out_weight, group_widths, pad_tokens):
    n = lax.axis_size("ctx")
    window = n // 2
    group_index = lax.axis_index("ctx")
    rows_here = queries.shape[0]
    heads_kv = keys.shape[1] // HEAD_SIZE
    context_group = queries.shape[1] // keys.shape[1]

    slots, uses, shift = gather_window(jnp.stack([keys, values]), n, window)

    prompt_ids = jnp.arange(group_widths.shape[0], dtype=jnp.int32)
    offsets = jnp.sum(
        jnp.where(prompt_ids[None, :] < prompt_ids[:, None], group_widths[None, :], 0), axis=1
    )
    owner = jnp.sum((offsets <= group_index).astype(jnp.int32)) - 1
    picked = prompt_ids == owner
    start = jnp.sum(jnp.where(picked, offsets, 0))
    width = jnp.sum(jnp.where(picked, group_widths, 0))
    padding = jnp.sum(jnp.where(picked, pad_tokens, 0))
    length = width * rows_here - padding
    local_rows = jnp.arange(rows_here, dtype=jnp.int32)
    query_pos = (group_index - start) * rows_here + local_rows
    key_pos = ((group_index - shift - start) * rows_here)[:, None] + local_rows[None, :]
    key_pos = key_pos.reshape(-1)

    usable = (key_pos >= 0) & (key_pos < length)
    key_limit = jnp.where(usable, key_pos, FAR * rows_here).reshape(1, -1)

    n_tp = lax.axis_size("tp")
    if n_tp == 2:
        me = lax.axis_index("tp")
        attended, peer_terms = attend(
            query_pos, key_pos, key_limit, queries, slots, uses, heads_kv, out_weight, 1 - me
        )
        got = lax.ppermute(peer_terms, "tp", [(0, 1), (1, 0)])
        part = out_weight.shape[1] // 2
        own_weight = lax.dynamic_slice_in_dim(out_weight, me * part, part, 1)
        own_terms = jnp.dot(attended, own_weight, preferred_element_type=jnp.float32)
        own_terms = lax.optimization_barrier(own_terms.astype(jnp.bfloat16)).astype(jnp.float32)
        return (own_terms + got.astype(jnp.float32)).astype(jnp.bfloat16)
    (attended,) = attend(query_pos, key_pos, key_limit, queries, slots, uses, heads_kv, None, jnp.int32(0))
    terms = jnp.dot(attended, out_weight, preferred_element_type=jnp.float32)
    return lax.psum_scatter(terms.astype(jnp.bfloat16), "tp", scatter_dimension=1, tiled=True)


def solution(mesh):
    return jax.shard_map(
        on_device,
        mesh=mesh,
        in_specs=(P("ctx", "tp"), P("ctx", "tp"), P("ctx", "tp"), P("tp", None), P(), P()),
        out_specs=P("ctx", "tp"),
        check_vma=False,
    )
```

```python
import functools
import math

import jax
import jax.numpy as jnp
from jax import lax
from jax.experimental import pallas as pl
from jax.experimental.pallas import tpu as pltpu
from jax.sharding import PartitionSpec as P

HEAD_SIZE = 128
FAR = 1 << 20


def gather_window(kv, n, window):
    received = []
    for s in range(1, window, 2):
        if s == 1:
            pairs = [(j, j + 1) for j in range(1, n - 1, 2)]
        else:
            pairs = [(j, j + s) for j in range(n - s)]
        received.append(lax.ppermute(kv, "ctx", pairs))
    across = [(j, j ^ 1) for j in range(n)]
    passed = [lax.ppermute(block, "ctx", across) for block in [kv] + received[:-1]]

    def pass_last(block):
        return lax.ppermute(block, "ctx", across)

    half = window // 2
    even_shift = [0] + [2 * m + 1 for m in range(half)] + [FAR, FAR] + [2 * m for m in range(1, half)]
    odd_shift = [0, FAR] + [2 * m + 1 for m in range(1, half)] + [1] + [2 * m + 2 for m in range(half)]
    core = lax.axis_index("ctx") % 2
    shift = jnp.where(core == 0, jnp.array(even_shift, jnp.int32), jnp.array(odd_shift, jnp.int32))
    return [kv] + received + passed, shift, pass_last


def turn(rows, cosine, sine):
    rows = rows.astype(jnp.float32)
    return (rows * cosine + pltpu.roll(rows, HEAD_SIZE // 2, 1) * sine).astype(jnp.bfloat16)


def attention_kernel(n_slots, heads_kv, late, project, peer_ref, query_pos_ref, key_limit_ref,
                     query_cos_ref, query_sin_ref, key_cos_ref, key_sin_ref, query_ref, *refs):
    if late:
        acc_in_ref, max_in_ref, sum_in_ref = refs[:3]
        refs = refs[3:]
    slot_refs = refs[:n_slots]
    rest = refs[n_slots:]
    if project:
        weight_hbm, out_ref, peer_out_ref, weight_ref, copy_sem = rest
        group = query_ref.shape[1] // heads_kv
        part = weight_ref.shape[1]
        copies = [
            pltpu.make_async_copy(
                weight_hbm.at[pl.ds(h * group, group), pl.ds(pl.multiple_of(peer_ref[0] * part, part), part)],
                weight_ref.at[pl.ds(h * group, group), :],
                copy_sem.at[h],
            )
            for h in range(heads_kv)
        ]
        for copy in copies:
            copy.start()
    elif late:
        (out_ref,) = rest
    else:
        acc_ref, max_ref, sum_ref = rest
    allowed = key_limit_ref[...] <= query_pos_ref[...]
    heads_here = query_ref.shape[1] // HEAD_SIZE // heads_kv
    for h in range(heads_kv):
        head = slice(h * HEAD_SIZE, (h + 1) * HEAD_SIZE)
        keys = turn(jnp.concatenate([r[0, :, head] for r in slot_refs], axis=0), key_cos_ref[...], key_sin_ref[...])
        values = jnp.concatenate([r[1, :, head] for r in slot_refs], axis=0)
        for g in range(heads_here):
            q = h * heads_here + g
            columns = slice(q * HEAD_SIZE, (q + 1) * HEAD_SIZE)
            query = turn(query_ref[:, columns], query_cos_ref[...], query_sin_ref[...])
            scores = lax.dot_general(
                query, keys, (((1,), (1,)), ((), ())), preferred_element_type=jnp.float32
            ) * (1.0 / math.sqrt(HEAD_SIZE))
            scores = jnp.where(allowed, scores, -1e30)
            highest = jnp.max(scores, axis=1, keepdims=True)
            if late:
                before = max_in_ref[:, q:q + 1]
                highest = jnp.maximum(before, highest)
                factor = jnp.exp(before - highest)
            weights = jnp.exp(scores - highest)
            totals = jnp.sum(weights, axis=1, keepdims=True)
            summed = jnp.dot(weights.astype(jnp.bfloat16), values, preferred_element_type=jnp.float32)
            if late:
                totals = sum_in_ref[:, q:q + 1] * factor + totals
                summed = acc_in_ref[:, columns] * factor + summed
                out_ref[:, columns] = (summed / totals).astype(out_ref.dtype)
            else:
                acc_ref[:, columns] = summed
                max_ref[:, q:q + 1] = highest
                sum_ref[:, q:q + 1] = totals
    if project:
        total = None
        for h in range(heads_kv):
            copies[h].wait()
            rows = slice(h * group, (h + 1) * group)
            term = jnp.dot(out_ref[:, rows], weight_ref[rows, :], preferred_element_type=jnp.float32)
            total = term if total is None else total + term
        peer_out_ref[...] = total.astype(peer_out_ref.dtype)


def tables(positions):
    half = HEAD_SIZE // 2
    freqs = 500000.0 ** (-jnp.arange(half, dtype=jnp.float32) / half)
    angles = positions.astype(jnp.float32)[:, None] * freqs[None, :]
    cosine = jnp.cos(angles)
    sine = jnp.sin(angles)
    return jnp.concatenate([cosine, cosine], axis=1), jnp.concatenate([-sine, sine], axis=1)


def attend(query_pos, key_pos, key_limit, queries, slots, heads_kv, carry=None, out_weight=None, peer=None):
    rows, width = queries.shape
    n_slots = len(slots)
    count = key_pos.shape[0]
    late = carry is not None
    project = out_weight is not None
    query_cos, query_sin = tables(query_pos)
    key_cos, key_sin = tables(key_pos)
    vmem = pl.BlockSpec(memory_space=pltpu.VMEM)
    smem = pl.BlockSpec(memory_space=pltpu.SMEM)
    args = [peer.reshape(1), query_pos.reshape(rows, 1), key_limit, query_cos, query_sin, key_cos, key_sin, queries]
    if late:
        args += list(carry)
    args += slots
    in_specs = [smem] + [vmem] * (len(args) - 1)
    heads = width // HEAD_SIZE
    if late:
        out_shape = [jax.ShapeDtypeStruct((rows, width), jnp.bfloat16)]
    else:
        out_shape = [jax.ShapeDtypeStruct((rows, width), jnp.float32),
                     jax.ShapeDtypeStruct((rows, heads), jnp.float32),
                     jax.ShapeDtypeStruct((rows, heads), jnp.float32)]
    scratch = []
    flops = 4 * rows * count * width
    moved = 2 * (2 * rows * width + 2 * count * heads_kv * HEAD_SIZE)
    if project:
        part = out_weight.shape[1] // 2
        args.append(out_weight)
        in_specs.append(pl.BlockSpec(memory_space=pl.ANY))
        out_shape.append(jax.ShapeDtypeStruct((rows, part), jnp.bfloat16))
        scratch += [pltpu.VMEM((width, part), jnp.bfloat16), pltpu.SemaphoreType.DMA((heads_kv,))]
        flops += 2 * rows * width * part
        moved += 2 * (width * part + rows * part)
    return pl.pallas_call(
        functools.partial(attention_kernel, n_slots, heads_kv, late, project),
        out_shape=out_shape,
        in_specs=in_specs,
        out_specs=[vmem] * len(out_shape),
        scratch_shapes=scratch,
        compiler_params=pltpu.CompilerParams(vmem_limit_bytes=48 * 1024 * 1024),
        cost_estimate=pl.CostEstimate(
            flops=flops, transcendentals=rows * count * width // HEAD_SIZE, bytes_accessed=moved
        ),
    )(*args)


def on_device(queries, keys, values, out_weight, group_widths, pad_tokens):
    n = lax.axis_size("ctx")
    window = n // 2
    group_index = lax.axis_index("ctx")
    rows_here = queries.shape[0]
    heads_kv = keys.shape[1] // HEAD_SIZE
    context_group = queries.shape[1] // keys.shape[1]

    slots, shift, pass_last = gather_window(jnp.stack([keys, values]), n, window)
    half = window // 2
    latest = [half, 2 * half + 1]
    early = [j for j in range(2 * half + 2) if j not in latest]

    prompt_ids = jnp.arange(group_widths.shape[0], dtype=jnp.int32)
    offsets = jnp.sum(
        jnp.where(prompt_ids[None, :] < prompt_ids[:, None], group_widths[None, :], 0), axis=1
    )
    owner = jnp.sum((offsets <= group_index).astype(jnp.int32)) - 1
    picked = prompt_ids == owner
    start = jnp.sum(jnp.where(picked, offsets, 0))
    width = jnp.sum(jnp.where(picked, group_widths, 0))
    padding = jnp.sum(jnp.where(picked, pad_tokens, 0))
    length = width * rows_here - padding
    local_rows = jnp.arange(rows_here, dtype=jnp.int32)
    query_pos = (group_index - start) * rows_here + local_rows

    def keys_at(chosen):
        key_pos = ((group_index - shift[jnp.array(chosen)] - start) * rows_here)[:, None] + local_rows[None, :]
        key_pos = key_pos.reshape(-1)
        usable = (key_pos >= 0) & (key_pos < length)
        return key_pos, jnp.where(usable, key_pos, FAR * rows_here).reshape(1, -1)

    zero = jnp.int32(0)
    carry = attend(query_pos, *keys_at(early), queries, [slots[j] for j in early], heads_kv, peer=zero)
    newest, carry = lax.optimization_barrier((slots[half], carry))
    last_slots = [newest, pass_last(newest)]

    n_tp = lax.axis_size("tp")
    if n_tp == 2:
        me = lax.axis_index("tp")
        attended, peer_terms = attend(
            query_pos, *keys_at(latest), queries, last_slots, heads_kv, carry=carry, out_weight=out_weight,
            peer=1 - me,
        )
        got = lax.ppermute(peer_terms, "tp", [(0, 1), (1, 0)])
        part = out_weight.shape[1] // 2
        own_weight = lax.dynamic_slice_in_dim(out_weight, me * part, part, 1)
        own_terms = jnp.dot(attended, own_weight, preferred_element_type=jnp.float32)
        own_terms = lax.optimization_barrier(own_terms.astype(jnp.bfloat16)).astype(jnp.float32)
        return (own_terms + got.astype(jnp.float32)).astype(jnp.bfloat16)
    (attended,) = attend(query_pos, *keys_at(latest), queries, last_slots, heads_kv, carry=carry, peer=zero)
    terms = jnp.dot(attended, out_weight, preferred_element_type=jnp.float32)
    return lax.psum_scatter(terms.astype(jnp.bfloat16), "tp", scatter_dimension=1, tiled=True)


def solution(mesh):
    return jax.shard_map(
        on_device,
        mesh=mesh,
        in_specs=(P("ctx", "tp"), P("ctx", "tp"), P("ctx", "tp"), P("tp", None), P(), P()),
        out_specs=P("ctx", "tp"),
        check_vma=False,
    )
```

```python
import functools
import math

import jax
import jax.numpy as jnp
from jax import lax
from jax.experimental import pallas as pl
from jax.experimental.pallas import tpu as pltpu
from jax.sharding import PartitionSpec as P

HEAD_SIZE = 128
FAR = 1 << 20


def gather_window(kv, n, window):
    received = []
    for s in range(1, window, 2):
        if s == 1:
            pairs = [(j, j + 1) for j in range(1, n - 1, 2)]
        else:
            pairs = [(j, j + s) for j in range(n - s)]
        received.append(lax.ppermute(kv, "ctx", pairs))
    across = [(j, j ^ 1) for j in range(n)]
    passed = [lax.ppermute(block, "ctx", across) for block in [kv] + received]
    half = window // 2
    even_shift = [0] + [2 * m + 1 for m in range(half)] + [FAR, FAR] + [2 * m for m in range(1, half)]
    odd_shift = [0, FAR] + [2 * m + 1 for m in range(1, half)] + [1] + [2 * m + 2 for m in range(half)]
    core = lax.axis_index("ctx") % 2
    shift = jnp.where(core == 0, jnp.array(even_shift, jnp.int32), jnp.array(odd_shift, jnp.int32))
    return [kv] + received + passed, shift


def turn(rows, cosine, sine):
    rows = rows.astype(jnp.float32)
    return (rows * cosine + pltpu.roll(rows, HEAD_SIZE // 2, 1) * sine).astype(jnp.bfloat16)


def attention_kernel(n_slots, uses, heads_kv, project, peer_ref, core_ref, query_pos_ref, key_limit_ref,
                     query_cos_ref, query_sin_ref, key_cos_ref, key_sin_ref, query_ref, *refs):
    slot_refs = refs[:n_slots]
    if project:
        weight_hbm, out_ref, peer_out_ref, weight_ref, copy_sem = refs[n_slots:]
        group = query_ref.shape[1] // heads_kv
        part = weight_ref.shape[1]
        copies = [
            pltpu.make_async_copy(
                weight_hbm.at[pl.ds(h * group, group), pl.ds(pl.multiple_of(peer_ref[0] * part, part), part)],
                weight_ref.at[pl.ds(h * group, group), :],
                copy_sem.at[h],
            )
            for h in range(heads_kv)
        ]
        for copy in copies:
            copy.start()
    else:
        (out_ref,) = refs[n_slots:]
    allowed = key_limit_ref[...] <= query_pos_ref[...]
    heads_here = query_ref.shape[1] // HEAD_SIZE // heads_kv

    def body(use):
        for h in range(heads_kv):
            head = slice(h * HEAD_SIZE, (h + 1) * HEAD_SIZE)
            keys = turn(jnp.concatenate([slot_refs[j][0, :, head] for j in use], axis=0),
                        key_cos_ref[...], key_sin_ref[...])
            values = jnp.concatenate([slot_refs[j][1, :, head] for j in use], axis=0)
            for g in range(heads_here):
                q = h * heads_here + g
                columns = slice(q * HEAD_SIZE, (q + 1) * HEAD_SIZE)
                query = turn(query_ref[:, columns], query_cos_ref[...], query_sin_ref[...])
                scores = lax.dot_general(
                    query, keys, (((1,), (1,)), ((), ())), preferred_element_type=jnp.float32
                )
                scores = jnp.where(allowed, scores, -1e30)
                highest = jnp.max(scores, axis=1, keepdims=True)
                weights = jnp.exp2((scores - highest) * (math.log2(math.e) / math.sqrt(HEAD_SIZE)))
                totals = jnp.sum(weights, axis=1, keepdims=True)
                summed = jnp.dot(weights.astype(jnp.bfloat16), values, preferred_element_type=jnp.float32)
                out_ref[:, columns] = (summed / totals).astype(out_ref.dtype)

    body(uses)
    if project:
        total = None
        for h in range(heads_kv):
            copies[h].wait()
            rows = slice(h * group, (h + 1) * group)
            term = jnp.dot(out_ref[:, rows], weight_ref[rows, :], preferred_element_type=jnp.float32)
            total = term if total is None else total + term
        peer_out_ref[...] = total.astype(peer_out_ref.dtype)


def tables(positions):
    half = HEAD_SIZE // 2
    freqs = 500000.0 ** (-jnp.arange(half, dtype=jnp.float32) / half)
    angles = positions.astype(jnp.float32)[:, None] * freqs[None, :]
    cosine = jnp.cos(angles)
    sine = jnp.sin(angles)
    return jnp.concatenate([cosine, cosine], axis=1), jnp.concatenate([-sine, sine], axis=1)


def attend(query_pos, key_pos, key_limit, queries, slots, uses, heads_kv, out_weight, peer):
    rows, width = queries.shape
    n_slots = len(slots)
    count = key_pos.shape[0]
    project = out_weight is not None
    query_cos, query_sin = tables(query_pos)
    key_cos, key_sin = tables(key_pos)
    vmem = pl.BlockSpec(memory_space=pltpu.VMEM)
    smem = pl.BlockSpec(memory_space=pltpu.SMEM)
    core = (lax.axis_index("ctx") % 2).astype(jnp.int32)
    args = [peer.reshape(1), core.reshape(1), query_pos.reshape(rows, 1), key_limit, query_cos, query_sin,
            key_cos, key_sin, queries] + slots
    in_specs = [smem, smem] + [vmem] * (7 + n_slots)
    out_shape = [jax.ShapeDtypeStruct((rows, width), jnp.bfloat16)]
    out_specs = [vmem]
    scratch = []
    flops = 4 * rows * count * width
    moved = 2 * (2 * rows * width + 2 * count * heads_kv * HEAD_SIZE)
    if project:
        part = out_weight.shape[1] // 2
        args.append(out_weight)
        in_specs.append(pl.BlockSpec(memory_space=pl.ANY))
        out_shape.append(jax.ShapeDtypeStruct((rows, part), jnp.bfloat16))
        out_specs.append(vmem)
        scratch += [pltpu.VMEM((width, part), jnp.bfloat16), pltpu.SemaphoreType.DMA((heads_kv,))]
        flops += 2 * rows * width * part
        moved += 2 * (width * part + rows * part)
    return pl.pallas_call(
        functools.partial(attention_kernel, n_slots, uses, heads_kv, project),
        out_shape=out_shape,
        in_specs=in_specs,
        out_specs=out_specs,
        scratch_shapes=scratch,
        compiler_params=pltpu.CompilerParams(vmem_limit_bytes=48 * 1024 * 1024),
        cost_estimate=pl.CostEstimate(
            flops=flops, transcendentals=rows * count * width // HEAD_SIZE, bytes_accessed=moved
        ),
    )(*args)


def on_device(queries, keys, values, out_weight, group_widths, pad_tokens):
    n = lax.axis_size("ctx")
    window = n // 2
    group_index = lax.axis_index("ctx")
    rows_here = queries.shape[0]
    heads_kv = keys.shape[1] // HEAD_SIZE
    context_group = queries.shape[1] // keys.shape[1]

    slots, shift = gather_window(jnp.stack([keys, values]), n, window)

    prompt_ids = jnp.arange(group_widths.shape[0], dtype=jnp.int32)
    offsets = jnp.sum(
        jnp.where(prompt_ids[None, :] < prompt_ids[:, None], group_widths[None, :], 0), axis=1
    )
    owner = jnp.sum((offsets <= group_index).astype(jnp.int32)) - 1
    picked = prompt_ids == owner
    start = jnp.sum(jnp.where(picked, offsets, 0))
    width = jnp.sum(jnp.where(picked, group_widths, 0))
    padding = jnp.sum(jnp.where(picked, pad_tokens, 0))
    length = width * rows_here - padding
    local_rows = jnp.arange(rows_here, dtype=jnp.int32)
    query_pos = (group_index - start) * rows_here + local_rows
    key_pos = ((group_index - shift - start) * rows_here)[:, None] + local_rows[None, :]
    key_pos = key_pos.reshape(-1)

    usable = (key_pos >= 0) & (key_pos < length)
    key_limit = jnp.where(usable, key_pos, FAR * rows_here).reshape(1, -1)

    n_tp = lax.axis_size("tp")
    if n_tp == 2:
        me = lax.axis_index("tp")
        attended, peer_terms = attend(
            query_pos, key_pos, key_limit, queries, slots, list(range(len(slots))), heads_kv, out_weight, 1 - me
        )
        got = lax.ppermute(peer_terms, "tp", [(0, 1), (1, 0)])
        part = out_weight.shape[1] // 2
        own_weight = lax.dynamic_slice_in_dim(out_weight, me * part, part, 1)
        own_terms = jnp.dot(attended, own_weight, preferred_element_type=jnp.float32)
        own_terms = lax.optimization_barrier(own_terms.astype(jnp.bfloat16)).astype(jnp.float32)
        return (own_terms + got.astype(jnp.float32)).astype(jnp.bfloat16)
    (attended,) = attend(query_pos, key_pos, key_limit, queries, slots, list(range(len(slots))), heads_kv, None, jnp.int32(0))
    terms = jnp.dot(attended, out_weight, preferred_element_type=jnp.float32)
    return lax.psum_scatter(terms.astype(jnp.bfloat16), "tp", scatter_dimension=1, tiled=True)


def solution(mesh):
    return jax.shard_map(
        on_device,
        mesh=mesh,
        in_specs=(P("ctx", "tp"), P("ctx", "tp"), P("ctx", "tp"), P("tp", None), P(), P()),
        out_specs=P("ctx", "tp"),
        check_vma=False,
    )
```

```python
import functools
import math

import jax
import jax.numpy as jnp
from jax import lax
from jax.experimental import pallas as pl
from jax.experimental.pallas import tpu as pltpu
from jax.sharding import PartitionSpec as P

HEAD_SIZE = 128
FAR = 1 << 20


def gather_window(kv, n, window):
    received = []
    for s in range(1, window, 2):
        if s == 1:
            pairs = [(j, j + 1) for j in range(1, n - 1, 2)]
        else:
            pairs = [(j, j + s) for j in range(n - s)]
        received.append(lax.ppermute(kv, "ctx", pairs))
    across = [(j, j ^ 1) for j in range(n)]
    passed = [lax.ppermute(block, "ctx", across) for block in [kv] + received]
    half = window // 2
    even_shift = [0] + [2 * m + 1 for m in range(half)] + [FAR, FAR] + [2 * m for m in range(1, half)]
    odd_shift = [0, FAR] + [2 * m + 1 for m in range(1, half)] + [1] + [2 * m + 2 for m in range(half)]
    core = lax.axis_index("ctx") % 2
    shift = jnp.where(core == 0, jnp.array(even_shift, jnp.int32), jnp.array(odd_shift, jnp.int32))
    return [kv] + received + passed, shift


def turn(rows, cosine, sine):
    rows = rows.astype(jnp.float32)
    return (rows * cosine + pltpu.roll(rows, HEAD_SIZE // 2, 1) * sine).astype(jnp.bfloat16)


def attention_kernel(n_slots, uses, heads_kv, project, peer_ref, core_ref, query_pos_ref, key_limit_ref,
                     query_cos_ref, query_sin_ref, key_cos_ref, key_sin_ref, query_ref, *refs):
    slot_refs = refs[:n_slots]
    if project:
        weight_hbm, out_ref, peer_out_ref, weight_ref, copy_sem = refs[n_slots:]
        group = query_ref.shape[1] // heads_kv
        part = weight_ref.shape[1]
        copies = [
            pltpu.make_async_copy(
                weight_hbm.at[pl.ds(h * group, group), pl.ds(pl.multiple_of(peer_ref[0] * part, part), part)],
                weight_ref.at[pl.ds(h * group, group), :],
                copy_sem.at[h],
            )
            for h in range(heads_kv)
        ]
        for copy in copies:
            copy.start()
    else:
        (out_ref,) = refs[n_slots:]
    allowed = key_limit_ref[...] <= query_pos_ref[...]
    heads_here = query_ref.shape[1] // HEAD_SIZE // heads_kv

    def body(use):
        for h in range(heads_kv):
            head = slice(h * HEAD_SIZE, (h + 1) * HEAD_SIZE)
            keys = turn(jnp.concatenate([slot_refs[j][0, :, head] for j in use], axis=0),
                        key_cos_ref[...], key_sin_ref[...]).T
            values = jnp.concatenate([slot_refs[j][1, :, head] for j in use], axis=0)
            for g in range(heads_here):
                q = h * heads_here + g
                columns = slice(q * HEAD_SIZE, (q + 1) * HEAD_SIZE)
                query = turn(query_ref[:, columns], query_cos_ref[...], query_sin_ref[...])
                scores = jnp.dot(query, keys, preferred_element_type=jnp.float32) * (1.0 / math.sqrt(HEAD_SIZE))
                scores = jnp.where(allowed, scores, -1e30)
                highest = jnp.max(scores, axis=1, keepdims=True)
                weights = jnp.exp(scores - highest)
                totals = jnp.sum(weights, axis=1, keepdims=True)
                summed = jnp.dot(weights.astype(jnp.bfloat16), values, preferred_element_type=jnp.float32)
                out_ref[:, columns] = (summed / totals).astype(out_ref.dtype)

    body(uses)
    if project:
        total = None
        for h in range(heads_kv):
            copies[h].wait()
            rows = slice(h * group, (h + 1) * group)
            term = jnp.dot(out_ref[:, rows], weight_ref[rows, :], preferred_element_type=jnp.float32)
            total = term if total is None else total + term
        peer_out_ref[...] = total.astype(peer_out_ref.dtype)


def tables(positions):
    half = HEAD_SIZE // 2
    freqs = 500000.0 ** (-jnp.arange(half, dtype=jnp.float32) / half)
    angles = positions.astype(jnp.float32)[:, None] * freqs[None, :]
    cosine = jnp.cos(angles)
    sine = jnp.sin(angles)
    return jnp.concatenate([cosine, cosine], axis=1), jnp.concatenate([-sine, sine], axis=1)


def attend(query_pos, key_pos, key_limit, queries, slots, uses, heads_kv, out_weight, peer):
    rows, width = queries.shape
    n_slots = len(slots)
    count = key_pos.shape[0]
    project = out_weight is not None
    query_cos, query_sin = tables(query_pos)
    key_cos, key_sin = tables(key_pos)
    vmem = pl.BlockSpec(memory_space=pltpu.VMEM)
    smem = pl.BlockSpec(memory_space=pltpu.SMEM)
    core = (lax.axis_index("ctx") % 2).astype(jnp.int32)
    args = [peer.reshape(1), core.reshape(1), query_pos.reshape(rows, 1), key_limit, query_cos, query_sin,
            key_cos, key_sin, queries] + slots
    in_specs = [smem, smem] + [vmem] * (7 + n_slots)
    out_shape = [jax.ShapeDtypeStruct((rows, width), jnp.bfloat16)]
    out_specs = [vmem]
    scratch = []
    flops = 4 * rows * count * width
    moved = 2 * (2 * rows * width + 2 * count * heads_kv * HEAD_SIZE)
    if project:
        part = out_weight.shape[1] // 2
        args.append(out_weight)
        in_specs.append(pl.BlockSpec(memory_space=pl.ANY))
        out_shape.append(jax.ShapeDtypeStruct((rows, part), jnp.bfloat16))
        out_specs.append(vmem)
        scratch += [pltpu.VMEM((width, part), jnp.bfloat16), pltpu.SemaphoreType.DMA((heads_kv,))]
        flops += 2 * rows * width * part
        moved += 2 * (width * part + rows * part)
    return pl.pallas_call(
        functools.partial(attention_kernel, n_slots, uses, heads_kv, project),
        out_shape=out_shape,
        in_specs=in_specs,
        out_specs=out_specs,
        scratch_shapes=scratch,
        compiler_params=pltpu.CompilerParams(vmem_limit_bytes=48 * 1024 * 1024),
        cost_estimate=pl.CostEstimate(
            flops=flops, transcendentals=rows * count * width // HEAD_SIZE, bytes_accessed=moved
        ),
    )(*args)


def on_device(queries, keys, values, out_weight, group_widths, pad_tokens):
    n = lax.axis_size("ctx")
    window = n // 2
    group_index = lax.axis_index("ctx")
    rows_here = queries.shape[0]
    heads_kv = keys.shape[1] // HEAD_SIZE
    context_group = queries.shape[1] // keys.shape[1]

    slots, shift = gather_window(jnp.stack([keys, values]), n, window)

    prompt_ids = jnp.arange(group_widths.shape[0], dtype=jnp.int32)
    offsets = jnp.sum(
        jnp.where(prompt_ids[None, :] < prompt_ids[:, None], group_widths[None, :], 0), axis=1
    )
    owner = jnp.sum((offsets <= group_index).astype(jnp.int32)) - 1
    picked = prompt_ids == owner
    start = jnp.sum(jnp.where(picked, offsets, 0))
    width = jnp.sum(jnp.where(picked, group_widths, 0))
    padding = jnp.sum(jnp.where(picked, pad_tokens, 0))
    length = width * rows_here - padding
    local_rows = jnp.arange(rows_here, dtype=jnp.int32)
    query_pos = (group_index - start) * rows_here + local_rows
    key_pos = ((group_index - shift - start) * rows_here)[:, None] + local_rows[None, :]
    key_pos = key_pos.reshape(-1)

    usable = (key_pos >= 0) & (key_pos < length)
    key_limit = jnp.where(usable, key_pos, FAR * rows_here).reshape(1, -1)

    n_tp = lax.axis_size("tp")
    if n_tp == 2:
        me = lax.axis_index("tp")
        attended, peer_terms = attend(
            query_pos, key_pos, key_limit, queries, slots, list(range(len(slots))), heads_kv, out_weight, 1 - me
        )
        got = lax.ppermute(peer_terms, "tp", [(0, 1), (1, 0)])
        part = out_weight.shape[1] // 2
        own_weight = lax.dynamic_slice_in_dim(out_weight, me * part, part, 1)
        own_terms = jnp.dot(attended, own_weight, preferred_element_type=jnp.float32)
        own_terms = lax.optimization_barrier(own_terms.astype(jnp.bfloat16)).astype(jnp.float32)
        return (own_terms + got.astype(jnp.float32)).astype(jnp.bfloat16)
    (attended,) = attend(query_pos, key_pos, key_limit, queries, slots, list(range(len(slots))), heads_kv, None, jnp.int32(0))
    terms = jnp.dot(attended, out_weight, preferred_element_type=jnp.float32)
    return lax.psum_scatter(terms.astype(jnp.bfloat16), "tp", scatter_dimension=1, tiled=True)


def solution(mesh):
    return jax.shard_map(
        on_device,
        mesh=mesh,
        in_specs=(P("ctx", "tp"), P("ctx", "tp"), P("ctx", "tp"), P("tp", None), P(), P()),
        out_specs=P("ctx", "tp"),
        check_vma=False,
    )
```

```python
import functools
import math

import jax
import jax.numpy as jnp
from jax import lax
from jax.experimental import pallas as pl
from jax.experimental.pallas import tpu as pltpu
from jax.sharding import PartitionSpec as P

HEAD_SIZE = 128
FAR = 1 << 20


def gather_window(kv, n, window):
    half = window // 2
    received = []
    for s in range(1, window, 2):
        received.append(lax.ppermute(kv, "ctx", [(j, j + s) for j in range(n - s)]))
    up = [(j, j + 1) for j in range(0, n, 2)]
    down = [(j + 1, j) for j in range(0, n, 2)]
    passed = []
    for m, block in enumerate(received):
        pairs = (up if m < half - 1 else []) + (down if m > 0 else [])
        passed.append(lax.ppermute(block, "ctx", pairs))
    even_shift = [0] + [2 * m + 1 for m in range(half)] + [FAR] + [2 * m for m in range(1, half)]
    odd_shift = [0] + [2 * m + 1 for m in range(half)] + [2 * m + 2 for m in range(half - 1)] + [FAR]
    core = lax.axis_index("ctx") % 2
    shift = jnp.where(core == 0, jnp.array(even_shift, jnp.int32), jnp.array(odd_shift, jnp.int32))
    return [kv] + received + passed, shift


def turn(rows, cosine, sine):
    rows = rows.astype(jnp.float32)
    return (rows * cosine + pltpu.roll(rows, HEAD_SIZE // 2, 1) * sine).astype(jnp.bfloat16)


def attention_kernel(n_slots, uses, heads_kv, project, peer_ref, core_ref, query_pos_ref, key_limit_ref,
                     query_cos_ref, query_sin_ref, key_cos_ref, key_sin_ref, query_ref, *refs):
    slot_refs = refs[:n_slots]
    if project:
        weight_hbm, out_ref, peer_out_ref, weight_ref, copy_sem = refs[n_slots:]
        group = query_ref.shape[1] // heads_kv
        part = weight_ref.shape[1]
        copies = [
            pltpu.make_async_copy(
                weight_hbm.at[pl.ds(h * group, group), pl.ds(pl.multiple_of(peer_ref[0] * part, part), part)],
                weight_ref.at[pl.ds(h * group, group), :],
                copy_sem.at[h],
            )
            for h in range(heads_kv)
        ]
        for copy in copies:
            copy.start()
    else:
        (out_ref,) = refs[n_slots:]
    allowed = key_limit_ref[...] <= query_pos_ref[...]
    heads_here = query_ref.shape[1] // HEAD_SIZE // heads_kv

    def body(use):
        for h in range(heads_kv):
            head = slice(h * HEAD_SIZE, (h + 1) * HEAD_SIZE)
            keys = turn(jnp.concatenate([slot_refs[j][0, :, head] for j in use], axis=0),
                        key_cos_ref[...], key_sin_ref[...])
            values = jnp.concatenate([slot_refs[j][1, :, head] for j in use], axis=0)
            for g in range(heads_here):
                q = h * heads_here + g
                columns = slice(q * HEAD_SIZE, (q + 1) * HEAD_SIZE)
                query = turn(query_ref[:, columns], query_cos_ref[...], query_sin_ref[...])
                scores = lax.dot_general(
                    query, keys, (((1,), (1,)), ((), ())), preferred_element_type=jnp.float32
                ) * (1.0 / math.sqrt(HEAD_SIZE))
                scores = jnp.where(allowed, scores, -1e30)
                highest = jnp.max(scores, axis=1, keepdims=True)
                weights = jnp.exp(scores - highest)
                totals = jnp.sum(weights, axis=1, keepdims=True)
                summed = jnp.dot(weights.astype(jnp.bfloat16), values, preferred_element_type=jnp.float32)
                out_ref[:, columns] = (summed / totals).astype(out_ref.dtype)

    body(uses)
    if project:
        total = None
        for h in range(heads_kv):
            copies[h].wait()
            rows = slice(h * group, (h + 1) * group)
            term = jnp.dot(out_ref[:, rows], weight_ref[rows, :], preferred_element_type=jnp.float32)
            total = term if total is None else total + term
        peer_out_ref[...] = total.astype(peer_out_ref.dtype)


def tables(positions):
    half = HEAD_SIZE // 2
    freqs = 500000.0 ** (-jnp.arange(half, dtype=jnp.float32) / half)
    angles = positions.astype(jnp.float32)[:, None] * freqs[None, :]
    cosine = jnp.cos(angles)
    sine = jnp.sin(angles)
    return jnp.concatenate([cosine, cosine], axis=1), jnp.concatenate([-sine, sine], axis=1)


def attend(query_pos, key_pos, key_limit, queries, slots, uses, heads_kv, out_weight, peer):
    rows, width = queries.shape
    n_slots = len(slots)
    count = key_pos.shape[0]
    project = out_weight is not None
    query_cos, query_sin = tables(query_pos)
    key_cos, key_sin = tables(key_pos)
    vmem = pl.BlockSpec(memory_space=pltpu.VMEM)
    smem = pl.BlockSpec(memory_space=pltpu.SMEM)
    core = (lax.axis_index("ctx") % 2).astype(jnp.int32)
    args = [peer.reshape(1), core.reshape(1), query_pos.reshape(rows, 1), key_limit, query_cos, query_sin,
            key_cos, key_sin, queries] + slots
    in_specs = [smem, smem] + [vmem] * (7 + n_slots)
    out_shape = [jax.ShapeDtypeStruct((rows, width), jnp.bfloat16)]
    out_specs = [vmem]
    scratch = []
    flops = 4 * rows * count * width
    moved = 2 * (2 * rows * width + 2 * count * heads_kv * HEAD_SIZE)
    if project:
        part = out_weight.shape[1] // 2
        args.append(out_weight)
        in_specs.append(pl.BlockSpec(memory_space=pl.ANY))
        out_shape.append(jax.ShapeDtypeStruct((rows, part), jnp.bfloat16))
        out_specs.append(vmem)
        scratch += [pltpu.VMEM((width, part), jnp.bfloat16), pltpu.SemaphoreType.DMA((heads_kv,))]
        flops += 2 * rows * width * part
        moved += 2 * (width * part + rows * part)
    return pl.pallas_call(
        functools.partial(attention_kernel, n_slots, uses, heads_kv, project),
        out_shape=out_shape,
        in_specs=in_specs,
        out_specs=out_specs,
        scratch_shapes=scratch,
        compiler_params=pltpu.CompilerParams(vmem_limit_bytes=48 * 1024 * 1024),
        cost_estimate=pl.CostEstimate(
            flops=flops, transcendentals=rows * count * width // HEAD_SIZE, bytes_accessed=moved
        ),
    )(*args)


def on_device(queries, keys, values, out_weight, group_widths, pad_tokens):
    n = lax.axis_size("ctx")
    window = n // 2
    group_index = lax.axis_index("ctx")
    rows_here = queries.shape[0]
    heads_kv = keys.shape[1] // HEAD_SIZE
    context_group = queries.shape[1] // keys.shape[1]

    slots, shift = gather_window(jnp.stack([keys, values]), n, window)

    prompt_ids = jnp.arange(group_widths.shape[0], dtype=jnp.int32)
    offsets = jnp.sum(
        jnp.where(prompt_ids[None, :] < prompt_ids[:, None], group_widths[None, :], 0), axis=1
    )
    owner = jnp.sum((offsets <= group_index).astype(jnp.int32)) - 1
    picked = prompt_ids == owner
    start = jnp.sum(jnp.where(picked, offsets, 0))
    width = jnp.sum(jnp.where(picked, group_widths, 0))
    padding = jnp.sum(jnp.where(picked, pad_tokens, 0))
    length = width * rows_here - padding
    local_rows = jnp.arange(rows_here, dtype=jnp.int32)
    query_pos = (group_index - start) * rows_here + local_rows
    key_pos = ((group_index - shift - start) * rows_here)[:, None] + local_rows[None, :]
    key_pos = key_pos.reshape(-1)

    usable = (key_pos >= 0) & (key_pos < length)
    key_limit = jnp.where(usable, key_pos, FAR * rows_here).reshape(1, -1)

    n_tp = lax.axis_size("tp")
    if n_tp == 2:
        me = lax.axis_index("tp")
        attended, peer_terms = attend(
            query_pos, key_pos, key_limit, queries, slots, list(range(len(slots))), heads_kv, out_weight, 1 - me
        )
        got = lax.ppermute(peer_terms, "tp", [(0, 1), (1, 0)])
        part = out_weight.shape[1] // 2
        own_weight = lax.dynamic_slice_in_dim(out_weight, me * part, part, 1)
        own_terms = jnp.dot(attended, own_weight, preferred_element_type=jnp.float32)
        own_terms = lax.optimization_barrier(own_terms.astype(jnp.bfloat16)).astype(jnp.float32)
        return (own_terms + got.astype(jnp.float32)).astype(jnp.bfloat16)
    (attended,) = attend(query_pos, key_pos, key_limit, queries, slots, list(range(len(slots))), heads_kv, None, jnp.int32(0))
    terms = jnp.dot(attended, out_weight, preferred_element_type=jnp.float32)
    return lax.psum_scatter(terms.astype(jnp.bfloat16), "tp", scatter_dimension=1, tiled=True)


def solution(mesh):
    return jax.shard_map(
        on_device,
        mesh=mesh,
        in_specs=(P("ctx", "tp"), P("ctx", "tp"), P("ctx", "tp"), P("tp", None), P(), P()),
        out_specs=P("ctx", "tp"),
        check_vma=False,
    )
```

```python
import functools
import math

import jax
import jax.numpy as jnp
from jax import lax
from jax.experimental import pallas as pl
from jax.experimental.pallas import tpu as pltpu
from jax.sharding import PartitionSpec as P

HEAD_SIZE = 128
FAR = 1 << 20


def gather_window(kv, n, window):
    half = window // 2
    received = []
    for s in range(1, window, 2):
        received.append(lax.ppermute(kv, "ctx", [(j, j + s) for j in range(n - s)]))
    up = [(j, j + 1) for j in range(0, n, 2)]
    down = [(j + 1, j) for j in range(0, n, 2)]
    passed = []
    for m, block in enumerate(received):
        pairs = up + (down if m > 0 else [])
        passed.append(lax.ppermute(block, "ctx", pairs))
    even_shift = [0] + [2 * m + 1 for m in range(half)] + [FAR] + [2 * m for m in range(1, half)]
    odd_shift = [0] + [2 * m + 1 for m in range(half)] + [2 * m + 2 for m in range(half - 1)] + [FAR]
    core = lax.axis_index("ctx") % 2
    shift = jnp.where(core == 0, jnp.array(even_shift, jnp.int32), jnp.array(odd_shift, jnp.int32))
    return [kv] + received + passed, shift


def turn(rows, cosine, sine):
    rows = rows.astype(jnp.float32)
    return (rows * cosine + pltpu.roll(rows, HEAD_SIZE // 2, 1) * sine).astype(jnp.bfloat16)


def attention_kernel(n_slots, uses, heads_kv, project, peer_ref, core_ref, query_pos_ref, key_limit_ref,
                     query_cos_ref, query_sin_ref, key_cos_ref, key_sin_ref, query_ref, *refs):
    slot_refs = refs[:n_slots]
    if project:
        weight_hbm, out_ref, peer_out_ref, weight_ref, copy_sem = refs[n_slots:]
        group = query_ref.shape[1] // heads_kv
        part = weight_ref.shape[1]
        copies = [
            pltpu.make_async_copy(
                weight_hbm.at[pl.ds(h * group, group), pl.ds(pl.multiple_of(peer_ref[0] * part, part), part)],
                weight_ref.at[pl.ds(h * group, group), :],
                copy_sem.at[h],
            )
            for h in range(heads_kv)
        ]
        for copy in copies:
            copy.start()
    else:
        (out_ref,) = refs[n_slots:]
    allowed = key_limit_ref[...] <= query_pos_ref[...]
    heads_here = query_ref.shape[1] // HEAD_SIZE // heads_kv

    def body(use):
        for h in range(heads_kv):
            head = slice(h * HEAD_SIZE, (h + 1) * HEAD_SIZE)
            keys = turn(jnp.concatenate([slot_refs[j][0, :, head] for j in use], axis=0),
                        key_cos_ref[...], key_sin_ref[...])
            values = jnp.concatenate([slot_refs[j][1, :, head] for j in use], axis=0)
            for g in range(heads_here):
                q = h * heads_here + g
                columns = slice(q * HEAD_SIZE, (q + 1) * HEAD_SIZE)
                query = turn(query_ref[:, columns], query_cos_ref[...], query_sin_ref[...])
                scores = lax.dot_general(
                    query, keys, (((1,), (1,)), ((), ())), preferred_element_type=jnp.float32
                ) * (1.0 / math.sqrt(HEAD_SIZE))
                scores = jnp.where(allowed, scores, -1e30)
                highest = jnp.max(scores, axis=1, keepdims=True)
                weights = jnp.exp(scores - highest)
                totals = jnp.sum(weights, axis=1, keepdims=True)
                summed = jnp.dot(weights.astype(jnp.bfloat16), values, preferred_element_type=jnp.float32)
                out_ref[:, columns] = (summed / totals).astype(out_ref.dtype)

    body(uses)
    if project:
        total = None
        for h in range(heads_kv):
            copies[h].wait()
            rows = slice(h * group, (h + 1) * group)
            term = jnp.dot(out_ref[:, rows], weight_ref[rows, :], preferred_element_type=jnp.float32)
            total = term if total is None else total + term
        peer_out_ref[...] = total.astype(peer_out_ref.dtype)


def tables(positions):
    half = HEAD_SIZE // 2
    freqs = 500000.0 ** (-jnp.arange(half, dtype=jnp.float32) / half)
    angles = positions.astype(jnp.float32)[:, None] * freqs[None, :]
    cosine = jnp.cos(angles)
    sine = jnp.sin(angles)
    return jnp.concatenate([cosine, cosine], axis=1), jnp.concatenate([-sine, sine], axis=1)


def attend(query_pos, key_pos, key_limit, queries, slots, uses, heads_kv, out_weight, peer):
    rows, width = queries.shape
    n_slots = len(slots)
    count = key_pos.shape[0]
    project = out_weight is not None
    query_cos, query_sin = tables(query_pos)
    key_cos, key_sin = tables(key_pos)
    vmem = pl.BlockSpec(memory_space=pltpu.VMEM)
    smem = pl.BlockSpec(memory_space=pltpu.SMEM)
    core = (lax.axis_index("ctx") % 2).astype(jnp.int32)
    args = [peer.reshape(1), core.reshape(1), query_pos.reshape(rows, 1), key_limit, query_cos, query_sin,
            key_cos, key_sin, queries] + slots
    in_specs = [smem, smem] + [vmem] * (7 + n_slots)
    out_shape = [jax.ShapeDtypeStruct((rows, width), jnp.bfloat16)]
    out_specs = [vmem]
    scratch = []
    flops = 4 * rows * count * width
    moved = 2 * (2 * rows * width + 2 * count * heads_kv * HEAD_SIZE)
    if project:
        part = out_weight.shape[1] // 2
        args.append(out_weight)
        in_specs.append(pl.BlockSpec(memory_space=pl.ANY))
        out_shape.append(jax.ShapeDtypeStruct((rows, part), jnp.bfloat16))
        out_specs.append(vmem)
        scratch += [pltpu.VMEM((width, part), jnp.bfloat16), pltpu.SemaphoreType.DMA((heads_kv,))]
        flops += 2 * rows * width * part
        moved += 2 * (width * part + rows * part)
    return pl.pallas_call(
        functools.partial(attention_kernel, n_slots, uses, heads_kv, project),
        out_shape=out_shape,
        in_specs=in_specs,
        out_specs=out_specs,
        scratch_shapes=scratch,
        compiler_params=pltpu.CompilerParams(vmem_limit_bytes=48 * 1024 * 1024),
        cost_estimate=pl.CostEstimate(
            flops=flops, transcendentals=rows * count * width // HEAD_SIZE, bytes_accessed=moved
        ),
    )(*args)


def on_device(queries, keys, values, out_weight, group_widths, pad_tokens):
    n = lax.axis_size("ctx")
    window = n // 2
    group_index = lax.axis_index("ctx")
    rows_here = queries.shape[0]
    heads_kv = keys.shape[1] // HEAD_SIZE
    context_group = queries.shape[1] // keys.shape[1]

    slots, shift = gather_window(jnp.stack([keys, values]), n, window)

    prompt_ids = jnp.arange(group_widths.shape[0], dtype=jnp.int32)
    offsets = jnp.sum(
        jnp.where(prompt_ids[None, :] < prompt_ids[:, None], group_widths[None, :], 0), axis=1
    )
    owner = jnp.sum((offsets <= group_index).astype(jnp.int32)) - 1
    picked = prompt_ids == owner
    start = jnp.sum(jnp.where(picked, offsets, 0))
    width = jnp.sum(jnp.where(picked, group_widths, 0))
    padding = jnp.sum(jnp.where(picked, pad_tokens, 0))
    length = width * rows_here - padding
    local_rows = jnp.arange(rows_here, dtype=jnp.int32)
    query_pos = (group_index - start) * rows_here + local_rows
    key_pos = ((group_index - shift - start) * rows_here)[:, None] + local_rows[None, :]
    key_pos = key_pos.reshape(-1)

    usable = (key_pos >= 0) & (key_pos < length)
    key_limit = jnp.where(usable, key_pos, FAR * rows_here).reshape(1, -1)

    n_tp = lax.axis_size("tp")
    if n_tp == 2:
        me = lax.axis_index("tp")
        attended, peer_terms = attend(
            query_pos, key_pos, key_limit, queries, slots, list(range(len(slots))), heads_kv, out_weight, 1 - me
        )
        got = lax.ppermute(peer_terms, "tp", [(0, 1), (1, 0)])
        part = out_weight.shape[1] // 2
        own_weight = lax.dynamic_slice_in_dim(out_weight, me * part, part, 1)
        own_terms = jnp.dot(attended, own_weight, preferred_element_type=jnp.float32)
        own_terms = lax.optimization_barrier(own_terms.astype(jnp.bfloat16)).astype(jnp.float32)
        return (own_terms + got.astype(jnp.float32)).astype(jnp.bfloat16)
    (attended,) = attend(query_pos, key_pos, key_limit, queries, slots, list(range(len(slots))), heads_kv, None, jnp.int32(0))
    terms = jnp.dot(attended, out_weight, preferred_element_type=jnp.float32)
    return lax.psum_scatter(terms.astype(jnp.bfloat16), "tp", scatter_dimension=1, tiled=True)


def solution(mesh):
    return jax.shard_map(
        on_device,
        mesh=mesh,
        in_specs=(P("ctx", "tp"), P("ctx", "tp"), P("ctx", "tp"), P("tp", None), P(), P()),
        out_specs=P("ctx", "tp"),
        check_vma=False,
    )
```

```python
import functools
import math

import jax
import jax.numpy as jnp
from jax import lax
from jax.experimental import pallas as pl
from jax.experimental.pallas import tpu as pltpu
from jax.sharding import PartitionSpec as P

HEAD_SIZE = 128
FAR = 1 << 20


def gather_window(kv, n, window):
    half = window // 2
    received = []
    for s in range(1, window, 2):
        received.append(lax.ppermute(kv, "ctx", [(j, j + s) for j in range(n - s)]))
    direct = lax.ppermute(kv, "ctx", [(j, j + window - 2) for j in range(0, n - window + 2, 2)])
    up = [(j, j + 1) for j in range(0, n, 2)]
    down = [(j + 1, j) for j in range(0, n, 2)]
    passed = []
    for m, block in enumerate(received[:-1]):
        passed.append(lax.ppermute(block, "ctx", up + (down if m > 0 else [])))
    even_shift = [0] + [2 * m + 1 for m in range(half)] + [FAR] + [2 * m for m in range(1, half - 1)] + [window - 2]
    odd_shift = [0] + [2 * m + 1 for m in range(half)] + [2 * m + 2 for m in range(half - 1)] + [FAR]
    core = lax.axis_index("ctx") % 2
    shift = jnp.where(core == 0, jnp.array(even_shift, jnp.int32), jnp.array(odd_shift, jnp.int32))
    return [kv] + received + passed + [direct], shift


def turn(rows, cosine, sine):
    rows = rows.astype(jnp.float32)
    return (rows * cosine + pltpu.roll(rows, HEAD_SIZE // 2, 1) * sine).astype(jnp.bfloat16)


def attention_kernel(n_slots, uses, heads_kv, project, peer_ref, core_ref, query_pos_ref, key_limit_ref,
                     query_cos_ref, query_sin_ref, key_cos_ref, key_sin_ref, query_ref, *refs):
    slot_refs = refs[:n_slots]
    if project:
        weight_hbm, out_ref, peer_out_ref, weight_ref, copy_sem = refs[n_slots:]
        group = query_ref.shape[1] // heads_kv
        part = weight_ref.shape[1]
        copies = [
            pltpu.make_async_copy(
                weight_hbm.at[pl.ds(h * group, group), pl.ds(pl.multiple_of(peer_ref[0] * part, part), part)],
                weight_ref.at[pl.ds(h * group, group), :],
                copy_sem.at[h],
            )
            for h in range(heads_kv)
        ]
        for copy in copies:
            copy.start()
    else:
        (out_ref,) = refs[n_slots:]
    allowed = key_limit_ref[...] <= query_pos_ref[...]
    heads_here = query_ref.shape[1] // HEAD_SIZE // heads_kv

    def body(use):
        for h in range(heads_kv):
            head = slice(h * HEAD_SIZE, (h + 1) * HEAD_SIZE)
            keys = turn(jnp.concatenate([slot_refs[j][0, :, head] for j in use], axis=0),
                        key_cos_ref[...], key_sin_ref[...])
            values = jnp.concatenate([slot_refs[j][1, :, head] for j in use], axis=0)
            for g in range(heads_here):
                q = h * heads_here + g
                columns = slice(q * HEAD_SIZE, (q + 1) * HEAD_SIZE)
                query = turn(query_ref[:, columns], query_cos_ref[...], query_sin_ref[...])
                scores = lax.dot_general(
                    query, keys, (((1,), (1,)), ((), ())), preferred_element_type=jnp.float32
                ) * (1.0 / math.sqrt(HEAD_SIZE))
                scores = jnp.where(allowed, scores, -1e30)
                highest = jnp.max(scores, axis=1, keepdims=True)
                weights = jnp.exp(scores - highest)
                totals = jnp.sum(weights, axis=1, keepdims=True)
                summed = jnp.dot(weights.astype(jnp.bfloat16), values, preferred_element_type=jnp.float32)
                out_ref[:, columns] = (summed / totals).astype(out_ref.dtype)

    body(uses)
    if project:
        total = None
        for h in range(heads_kv):
            copies[h].wait()
            rows = slice(h * group, (h + 1) * group)
            term = jnp.dot(out_ref[:, rows], weight_ref[rows, :], preferred_element_type=jnp.float32)
            total = term if total is None else total + term
        peer_out_ref[...] = total.astype(peer_out_ref.dtype)


def tables(positions):
    half = HEAD_SIZE // 2
    freqs = 500000.0 ** (-jnp.arange(half, dtype=jnp.float32) / half)
    angles = positions.astype(jnp.float32)[:, None] * freqs[None, :]
    cosine = jnp.cos(angles)
    sine = jnp.sin(angles)
    return jnp.concatenate([cosine, cosine], axis=1), jnp.concatenate([-sine, sine], axis=1)


def attend(query_pos, key_pos, key_limit, queries, slots, uses, heads_kv, out_weight, peer):
    rows, width = queries.shape
    n_slots = len(slots)
    count = key_pos.shape[0]
    project = out_weight is not None
    query_cos, query_sin = tables(query_pos)
    key_cos, key_sin = tables(key_pos)
    vmem = pl.BlockSpec(memory_space=pltpu.VMEM)
    smem = pl.BlockSpec(memory_space=pltpu.SMEM)
    core = (lax.axis_index("ctx") % 2).astype(jnp.int32)
    args = [peer.reshape(1), core.reshape(1), query_pos.reshape(rows, 1), key_limit, query_cos, query_sin,
            key_cos, key_sin, queries] + slots
    in_specs = [smem, smem] + [vmem] * (7 + n_slots)
    out_shape = [jax.ShapeDtypeStruct((rows, width), jnp.bfloat16)]
    out_specs = [vmem]
    scratch = []
    flops = 4 * rows * count * width
    moved = 2 * (2 * rows * width + 2 * count * heads_kv * HEAD_SIZE)
    if project:
        part = out_weight.shape[1] // 2
        args.append(out_weight)
        in_specs.append(pl.BlockSpec(memory_space=pl.ANY))
        out_shape.append(jax.ShapeDtypeStruct((rows, part), jnp.bfloat16))
        out_specs.append(vmem)
        scratch += [pltpu.VMEM((width, part), jnp.bfloat16), pltpu.SemaphoreType.DMA((heads_kv,))]
        flops += 2 * rows * width * part
        moved += 2 * (width * part + rows * part)
    return pl.pallas_call(
        functools.partial(attention_kernel, n_slots, uses, heads_kv, project),
        out_shape=out_shape,
        in_specs=in_specs,
        out_specs=out_specs,
        scratch_shapes=scratch,
        compiler_params=pltpu.CompilerParams(vmem_limit_bytes=48 * 1024 * 1024),
        cost_estimate=pl.CostEstimate(
            flops=flops, transcendentals=rows * count * width // HEAD_SIZE, bytes_accessed=moved
        ),
    )(*args)


def on_device(queries, keys, values, out_weight, group_widths, pad_tokens):
    n = lax.axis_size("ctx")
    window = n // 2
    group_index = lax.axis_index("ctx")
    rows_here = queries.shape[0]
    heads_kv = keys.shape[1] // HEAD_SIZE
    context_group = queries.shape[1] // keys.shape[1]

    slots, shift = gather_window(jnp.stack([keys, values]), n, window)

    prompt_ids = jnp.arange(group_widths.shape[0], dtype=jnp.int32)
    offsets = jnp.sum(
        jnp.where(prompt_ids[None, :] < prompt_ids[:, None], group_widths[None, :], 0), axis=1
    )
    owner = jnp.sum((offsets <= group_index).astype(jnp.int32)) - 1
    picked = prompt_ids == owner
    start = jnp.sum(jnp.where(picked, offsets, 0))
    width = jnp.sum(jnp.where(picked, group_widths, 0))
    padding = jnp.sum(jnp.where(picked, pad_tokens, 0))
    length = width * rows_here - padding
    local_rows = jnp.arange(rows_here, dtype=jnp.int32)
    query_pos = (group_index - start) * rows_here + local_rows
    key_pos = ((group_index - shift - start) * rows_here)[:, None] + local_rows[None, :]
    key_pos = key_pos.reshape(-1)

    usable = (key_pos >= 0) & (key_pos < length)
    key_limit = jnp.where(usable, key_pos, FAR * rows_here).reshape(1, -1)

    n_tp = lax.axis_size("tp")
    if n_tp == 2:
        me = lax.axis_index("tp")
        attended, peer_terms = attend(
            query_pos, key_pos, key_limit, queries, slots, list(range(len(slots))), heads_kv, out_weight, 1 - me
        )
        got = lax.ppermute(peer_terms, "tp", [(0, 1), (1, 0)])
        part = out_weight.shape[1] // 2
        own_weight = lax.dynamic_slice_in_dim(out_weight, me * part, part, 1)
        own_terms = jnp.dot(attended, own_weight, preferred_element_type=jnp.float32)
        own_terms = lax.optimization_barrier(own_terms.astype(jnp.bfloat16)).astype(jnp.float32)
        return (own_terms + got.astype(jnp.float32)).astype(jnp.bfloat16)
    (attended,) = attend(query_pos, key_pos, key_limit, queries, slots, list(range(len(slots))), heads_kv, None, jnp.int32(0))
    terms = jnp.dot(attended, out_weight, preferred_element_type=jnp.float32)
    return lax.psum_scatter(terms.astype(jnp.bfloat16), "tp", scatter_dimension=1, tiled=True)


def solution(mesh):
    return jax.shard_map(
        on_device,
        mesh=mesh,
        in_specs=(P("ctx", "tp"), P("ctx", "tp"), P("ctx", "tp"), P("tp", None), P(), P()),
        out_specs=P("ctx", "tp"),
        check_vma=False,
    )
```

```python
import functools
import math

import jax
import jax.numpy as jnp
from jax import lax
from jax.experimental import pallas as pl
from jax.experimental.pallas import tpu as pltpu
from jax.sharding import PartitionSpec as P

HEAD_SIZE = 128
FAR = 1 << 20


def gather_window(kv, n, window):
    half = window // 2
    received = []
    for s in range(1, window, 2):
        received.append(lax.ppermute(kv, "ctx", [(j, j + s) for j in range(n - s)]))
    up = [(j, j + 1) for j in range(0, n, 2)]
    down = [(j + 1, j) for j in range(0, n, 2)]
    passed = []
    for m, block in enumerate(received):
        pairs = up + (down if m > 0 else [])
        passed.append(lax.ppermute(block, "ctx", pairs))
    even_shift = [0] + [2 * m + 1 for m in range(half)] + [FAR] + [2 * m for m in range(1, half)]
    odd_shift = [0] + [2 * m + 1 for m in range(half)] + [2 * m + 2 for m in range(half - 1)] + [FAR]
    core = lax.axis_index("ctx") % 2
    shift = jnp.where(core == 0, jnp.array(even_shift, jnp.int32), jnp.array(odd_shift, jnp.int32))
    return [kv] + received + passed, shift


def turn(rows, cosine, sine):
    rows = rows.astype(jnp.float32)
    return (rows * cosine + pltpu.roll(rows, HEAD_SIZE // 2, 1) * sine).astype(jnp.bfloat16)


def attention_kernel(n_slots, uses, heads_kv, project, peer_ref, core_ref, query_pos_ref, key_limit_ref,
                     query_cos_ref, query_sin_ref, key_cos_ref, key_sin_ref, query_ref, *refs):
    slot_refs = refs[:n_slots]
    if project:
        weight_hbm, out_ref, peer_out_ref, weight_ref, copy_sem = refs[n_slots:]
        group = query_ref.shape[1] // heads_kv
        part = weight_ref.shape[1]
        copies = [
            pltpu.make_async_copy(
                weight_hbm.at[pl.ds(h * group, group), pl.ds(pl.multiple_of(peer_ref[0] * part, part), part)],
                weight_ref.at[pl.ds(h * group, group), :],
                copy_sem.at[h],
            )
            for h in range(heads_kv)
        ]
        for copy in copies:
            copy.start()
    else:
        (out_ref,) = refs[n_slots:]
    allowed = key_limit_ref[...] <= query_pos_ref[...]
    heads_here = query_ref.shape[1] // HEAD_SIZE // heads_kv

    def body(use):
        total = None
        for h in range(heads_kv):
            head = slice(h * HEAD_SIZE, (h + 1) * HEAD_SIZE)
            keys = turn(jnp.concatenate([slot_refs[j][0, :, head] for j in use], axis=0),
                        key_cos_ref[...], key_sin_ref[...])
            values = jnp.concatenate([slot_refs[j][1, :, head] for j in use], axis=0)
            for g in range(heads_here):
                q = h * heads_here + g
                columns = slice(q * HEAD_SIZE, (q + 1) * HEAD_SIZE)
                query = turn(query_ref[:, columns], query_cos_ref[...], query_sin_ref[...])
                scores = lax.dot_general(
                    query, keys, (((1,), (1,)), ((), ())), preferred_element_type=jnp.float32
                ) * (1.0 / math.sqrt(HEAD_SIZE))
                scores = jnp.where(allowed, scores, -1e30)
                highest = jnp.max(scores, axis=1, keepdims=True)
                weights = jnp.exp(scores - highest)
                totals = jnp.sum(weights, axis=1, keepdims=True)
                summed = jnp.dot(weights.astype(jnp.bfloat16), values, preferred_element_type=jnp.float32)
                out_ref[:, columns] = (summed / totals).astype(out_ref.dtype)
            if project:
                copies[h].wait()
                rows = slice(h * group, (h + 1) * group)
                term = jnp.dot(out_ref[:, rows], weight_ref[rows, :], preferred_element_type=jnp.float32)
                total = term if total is None else total + term
        if project:
            peer_out_ref[...] = total.astype(peer_out_ref.dtype)

    body(uses)


def tables(positions):
    half = HEAD_SIZE // 2
    freqs = 500000.0 ** (-jnp.arange(half, dtype=jnp.float32) / half)
    angles = positions.astype(jnp.float32)[:, None] * freqs[None, :]
    cosine = jnp.cos(angles)
    sine = jnp.sin(angles)
    return jnp.concatenate([cosine, cosine], axis=1), jnp.concatenate([-sine, sine], axis=1)


def attend(query_pos, key_pos, key_limit, queries, slots, uses, heads_kv, out_weight, peer):
    rows, width = queries.shape
    n_slots = len(slots)
    count = key_pos.shape[0]
    project = out_weight is not None
    query_cos, query_sin = tables(query_pos)
    key_cos, key_sin = tables(key_pos)
    vmem = pl.BlockSpec(memory_space=pltpu.VMEM)
    smem = pl.BlockSpec(memory_space=pltpu.SMEM)
    core = (lax.axis_index("ctx") % 2).astype(jnp.int32)
    args = [peer.reshape(1), core.reshape(1), query_pos.reshape(rows, 1), key_limit, query_cos, query_sin,
            key_cos, key_sin, queries] + slots
    in_specs = [smem, smem] + [vmem] * (7 + n_slots)
    out_shape = [jax.ShapeDtypeStruct((rows, width), jnp.bfloat16)]
    out_specs = [vmem]
    scratch = []
    flops = 4 * rows * count * width
    moved = 2 * (2 * rows * width + 2 * count * heads_kv * HEAD_SIZE)
    if project:
        part = out_weight.shape[1] // 2
        args.append(out_weight)
        in_specs.append(pl.BlockSpec(memory_space=pl.ANY))
        out_shape.append(jax.ShapeDtypeStruct((rows, part), jnp.bfloat16))
        out_specs.append(vmem)
        scratch += [pltpu.VMEM((width, part), jnp.bfloat16), pltpu.SemaphoreType.DMA((heads_kv,))]
        flops += 2 * rows * width * part
        moved += 2 * (width * part + rows * part)
    return pl.pallas_call(
        functools.partial(attention_kernel, n_slots, uses, heads_kv, project),
        out_shape=out_shape,
        in_specs=in_specs,
        out_specs=out_specs,
        scratch_shapes=scratch,
        compiler_params=pltpu.CompilerParams(vmem_limit_bytes=48 * 1024 * 1024),
        cost_estimate=pl.CostEstimate(
            flops=flops, transcendentals=rows * count * width // HEAD_SIZE, bytes_accessed=moved
        ),
    )(*args)


def on_device(queries, keys, values, out_weight, group_widths, pad_tokens):
    n = lax.axis_size("ctx")
    window = n // 2
    group_index = lax.axis_index("ctx")
    rows_here = queries.shape[0]
    heads_kv = keys.shape[1] // HEAD_SIZE
    context_group = queries.shape[1] // keys.shape[1]

    slots, shift = gather_window(jnp.stack([keys, values]), n, window)

    prompt_ids = jnp.arange(group_widths.shape[0], dtype=jnp.int32)
    offsets = jnp.sum(
        jnp.where(prompt_ids[None, :] < prompt_ids[:, None], group_widths[None, :], 0), axis=1
    )
    owner = jnp.sum((offsets <= group_index).astype(jnp.int32)) - 1
    picked = prompt_ids == owner
    start = jnp.sum(jnp.where(picked, offsets, 0))
    width = jnp.sum(jnp.where(picked, group_widths, 0))
    padding = jnp.sum(jnp.where(picked, pad_tokens, 0))
    length = width * rows_here - padding
    local_rows = jnp.arange(rows_here, dtype=jnp.int32)
    query_pos = (group_index - start) * rows_here + local_rows
    key_pos = ((group_index - shift - start) * rows_here)[:, None] + local_rows[None, :]
    key_pos = key_pos.reshape(-1)

    usable = (key_pos >= 0) & (key_pos < length)
    key_limit = jnp.where(usable, key_pos, FAR * rows_here).reshape(1, -1)

    n_tp = lax.axis_size("tp")
    if n_tp == 2:
        me = lax.axis_index("tp")
        attended, peer_terms = attend(
            query_pos, key_pos, key_limit, queries, slots, list(range(len(slots))), heads_kv, out_weight, 1 - me
        )
        got = lax.ppermute(peer_terms, "tp", [(0, 1), (1, 0)])
        part = out_weight.shape[1] // 2
        own_weight = lax.dynamic_slice_in_dim(out_weight, me * part, part, 1)
        own_terms = jnp.dot(attended, own_weight, preferred_element_type=jnp.float32)
        own_terms = lax.optimization_barrier(own_terms.astype(jnp.bfloat16)).astype(jnp.float32)
        return (own_terms + got.astype(jnp.float32)).astype(jnp.bfloat16)
    (attended,) = attend(query_pos, key_pos, key_limit, queries, slots, list(range(len(slots))), heads_kv, None, jnp.int32(0))
    terms = jnp.dot(attended, out_weight, preferred_element_type=jnp.float32)
    return lax.psum_scatter(terms.astype(jnp.bfloat16), "tp", scatter_dimension=1, tiled=True)


def solution(mesh):
    return jax.shard_map(
        on_device,
        mesh=mesh,
        in_specs=(P("ctx", "tp"), P("ctx", "tp"), P("ctx", "tp"), P("tp", None), P(), P()),
        out_specs=P("ctx", "tp"),
        check_vma=False,
    )
```

```python
import functools
import math

import jax
import jax.numpy as jnp
from jax import lax
from jax.experimental import pallas as pl
from jax.experimental.pallas import tpu as pltpu
from jax.sharding import PartitionSpec as P

HEAD_SIZE = 128
FAR = 1 << 20


def gather_window(kv, n, window):
    half = window // 2
    received = []
    for s in range(1, window, 2):
        received.append(lax.ppermute(kv, "ctx", [(j, j + s) for j in range(n - s)]))
    up = [(j, j + 1) for j in range(0, n, 2)]
    down = [(j + 1, j) for j in range(0, n, 2)]
    passed = []
    for m, block in enumerate(received):
        pairs = up + (down if m > 0 else [])
        passed.append(lax.ppermute(block, "ctx", pairs))
    even_shift = [0] + [2 * m + 1 for m in range(half)] + [FAR] + [2 * m for m in range(1, half)]
    odd_shift = [0] + [2 * m + 1 for m in range(half)] + [2 * m + 2 for m in range(half - 1)] + [FAR]
    core = lax.axis_index("ctx") % 2
    shift = jnp.where(core == 0, jnp.array(even_shift, jnp.int32), jnp.array(odd_shift, jnp.int32))
    return [kv] + received + passed, shift


def turn(rows, cosine, sine):
    rows = rows.astype(jnp.float32)
    return (rows * cosine + pltpu.roll(rows, HEAD_SIZE // 2, 1) * sine).astype(jnp.bfloat16)


def attention_kernel(n_slots, uses, heads_kv, project, peer_ref, core_ref, query_pos_ref, key_limit_ref,
                     query_cos_ref, query_sin_ref, key_cos_ref, key_sin_ref, query_ref, *refs):
    slot_refs = refs[:n_slots]
    if project:
        weight_hbm, out_ref, peer_out_ref, weight_ref, copy_sem = refs[n_slots:]
        group = query_ref.shape[1] // heads_kv
        part = weight_ref.shape[1]
        copies = [
            pltpu.make_async_copy(
                weight_hbm.at[pl.ds(h * group, group), pl.ds(pl.multiple_of(peer_ref[0] * part, part), part)],
                weight_ref.at[pl.ds(h * group, group), :],
                copy_sem.at[h],
            )
            for h in range(heads_kv)
        ]
        for copy in copies:
            copy.start()
    else:
        (out_ref,) = refs[n_slots:]
    allowed = key_limit_ref[...] <= query_pos_ref[...]
    heads_here = query_ref.shape[1] // HEAD_SIZE // heads_kv

    def body(use):
        total = None
        for h in range(heads_kv):
            head = slice(h * HEAD_SIZE, (h + 1) * HEAD_SIZE)
            keys = turn(jnp.concatenate([slot_refs[j][0, :, head] for j in use], axis=0),
                        key_cos_ref[...], key_sin_ref[...])
            values = jnp.concatenate([slot_refs[j][1, :, head] for j in use], axis=0)
            for g in range(heads_here):
                q = h * heads_here + g
                columns = slice(q * HEAD_SIZE, (q + 1) * HEAD_SIZE)
                query = turn(query_ref[:, columns], query_cos_ref[...], query_sin_ref[...])
                scores = lax.dot_general(
                    query, keys, (((1,), (1,)), ((), ())), preferred_element_type=jnp.float32
                ) * (1.0 / math.sqrt(HEAD_SIZE))
                scores = jnp.where(allowed, scores, -1e30)
                highest = jnp.max(scores, axis=1, keepdims=True)
                weights = jnp.exp(scores - highest)
                totals = jnp.sum(weights, axis=1, keepdims=True)
                summed = jnp.dot(weights.astype(jnp.bfloat16), values, preferred_element_type=jnp.float32)
                out_ref[:, columns] = (summed / totals).astype(out_ref.dtype)
            if project and (h % 2 == 1 or h == heads_kv - 1):
                done = range(h - h % 2, h + 1)
                for k in done:
                    copies[k].wait()
                for k in done:
                    rows = slice(k * group, (k + 1) * group)
                    term = jnp.dot(out_ref[:, rows], weight_ref[rows, :], preferred_element_type=jnp.float32)
                    total = term if total is None else total + term
        if project:
            peer_out_ref[...] = total.astype(peer_out_ref.dtype)

    body(uses)


def tables(positions):
    half = HEAD_SIZE // 2
    freqs = 500000.0 ** (-jnp.arange(half, dtype=jnp.float32) / half)
    angles = positions.astype(jnp.float32)[:, None] * freqs[None, :]
    cosine = jnp.cos(angles)
    sine = jnp.sin(angles)
    return jnp.concatenate([cosine, cosine], axis=1), jnp.concatenate([-sine, sine], axis=1)


def attend(query_pos, key_pos, key_limit, queries, slots, uses, heads_kv, out_weight, peer):
    rows, width = queries.shape
    n_slots = len(slots)
    count = key_pos.shape[0]
    project = out_weight is not None
    query_cos, query_sin = tables(query_pos)
    key_cos, key_sin = tables(key_pos)
    vmem = pl.BlockSpec(memory_space=pltpu.VMEM)
    smem = pl.BlockSpec(memory_space=pltpu.SMEM)
    core = (lax.axis_index("ctx") % 2).astype(jnp.int32)
    args = [peer.reshape(1), core.reshape(1), query_pos.reshape(rows, 1), key_limit, query_cos, query_sin,
            key_cos, key_sin, queries] + slots
    in_specs = [smem, smem] + [vmem] * (7 + n_slots)
    out_shape = [jax.ShapeDtypeStruct((rows, width), jnp.bfloat16)]
    out_specs = [vmem]
    scratch = []
    flops = 4 * rows * count * width
    moved = 2 * (2 * rows * width + 2 * count * heads_kv * HEAD_SIZE)
    if project:
        part = out_weight.shape[1] // 2
        args.append(out_weight)
        in_specs.append(pl.BlockSpec(memory_space=pl.ANY))
        out_shape.append(jax.ShapeDtypeStruct((rows, part), jnp.bfloat16))
        out_specs.append(vmem)
        scratch += [pltpu.VMEM((width, part), jnp.bfloat16), pltpu.SemaphoreType.DMA((heads_kv,))]
        flops += 2 * rows * width * part
        moved += 2 * (width * part + rows * part)
    return pl.pallas_call(
        functools.partial(attention_kernel, n_slots, uses, heads_kv, project),
        out_shape=out_shape,
        in_specs=in_specs,
        out_specs=out_specs,
        scratch_shapes=scratch,
        compiler_params=pltpu.CompilerParams(vmem_limit_bytes=48 * 1024 * 1024),
        cost_estimate=pl.CostEstimate(
            flops=flops, transcendentals=rows * count * width // HEAD_SIZE, bytes_accessed=moved
        ),
    )(*args)


def on_device(queries, keys, values, out_weight, group_widths, pad_tokens):
    n = lax.axis_size("ctx")
    window = n // 2
    group_index = lax.axis_index("ctx")
    rows_here = queries.shape[0]
    heads_kv = keys.shape[1] // HEAD_SIZE
    context_group = queries.shape[1] // keys.shape[1]

    slots, shift = gather_window(jnp.stack([keys, values]), n, window)

    prompt_ids = jnp.arange(group_widths.shape[0], dtype=jnp.int32)
    offsets = jnp.sum(
        jnp.where(prompt_ids[None, :] < prompt_ids[:, None], group_widths[None, :], 0), axis=1
    )
    owner = jnp.sum((offsets <= group_index).astype(jnp.int32)) - 1
    picked = prompt_ids == owner
    start = jnp.sum(jnp.where(picked, offsets, 0))
    width = jnp.sum(jnp.where(picked, group_widths, 0))
    padding = jnp.sum(jnp.where(picked, pad_tokens, 0))
    length = width * rows_here - padding
    local_rows = jnp.arange(rows_here, dtype=jnp.int32)
    query_pos = (group_index - start) * rows_here + local_rows
    key_pos = ((group_index - shift - start) * rows_here)[:, None] + local_rows[None, :]
    key_pos = key_pos.reshape(-1)

    usable = (key_pos >= 0) & (key_pos < length)
    key_limit = jnp.where(usable, key_pos, FAR * rows_here).reshape(1, -1)

    n_tp = lax.axis_size("tp")
    if n_tp == 2:
        me = lax.axis_index("tp")
        attended, peer_terms = attend(
            query_pos, key_pos, key_limit, queries, slots, list(range(len(slots))), heads_kv, out_weight, 1 - me
        )
        got = lax.ppermute(peer_terms, "tp", [(0, 1), (1, 0)])
        part = out_weight.shape[1] // 2
        own_weight = lax.dynamic_slice_in_dim(out_weight, me * part, part, 1)
        own_terms = jnp.dot(attended, own_weight, preferred_element_type=jnp.float32)
        own_terms = lax.optimization_barrier(own_terms.astype(jnp.bfloat16)).astype(jnp.float32)
        return (own_terms + got.astype(jnp.float32)).astype(jnp.bfloat16)
    (attended,) = attend(query_pos, key_pos, key_limit, queries, slots, list(range(len(slots))), heads_kv, None, jnp.int32(0))
    terms = jnp.dot(attended, out_weight, preferred_element_type=jnp.float32)
    return lax.psum_scatter(terms.astype(jnp.bfloat16), "tp", scatter_dimension=1, tiled=True)


def solution(mesh):
    return jax.shard_map(
        on_device,
        mesh=mesh,
        in_specs=(P("ctx", "tp"), P("ctx", "tp"), P("ctx", "tp"), P("tp", None), P(), P()),
        out_specs=P("ctx", "tp"),
        check_vma=False,
    )
```

```python
import functools
import math

import jax
import jax.numpy as jnp
from jax import lax
from jax.experimental import pallas as pl
from jax.experimental.pallas import tpu as pltpu
from jax.sharding import PartitionSpec as P

HEAD_SIZE = 128
FAR = 1 << 20


def gather_window(kv, n, window):
    half = window // 2
    received = []
    for s in range(1, window, 2):
        received.append(lax.ppermute(kv, "ctx", [(j, j + s) for j in range(n - s)]))
    up = [(j, j + 1) for j in range(0, n, 2)]
    down = [(j + 1, j) for j in range(0, n, 2)]
    passed = []
    for m, block in enumerate(received):
        pairs = up + (down if m > 0 else [])
        passed.append(lax.ppermute(block, "ctx", pairs))
    even_shift = [0] + [2 * m + 1 for m in range(half)] + [FAR] + [2 * m for m in range(1, half)]
    odd_shift = [0] + [2 * m + 1 for m in range(half)] + [2 * m + 2 for m in range(half - 1)] + [FAR]
    core = lax.axis_index("ctx") % 2
    shift = jnp.where(core == 0, jnp.array(even_shift, jnp.int32), jnp.array(odd_shift, jnp.int32))
    return [kv] + received + passed, shift


def turn(rows, cosine, sine):
    rows = rows.astype(jnp.float32)
    return (rows * cosine + pltpu.roll(rows, HEAD_SIZE // 2, 1) * sine).astype(jnp.bfloat16)


def attention_kernel(n_slots, uses, heads_kv, project, peer_ref, core_ref, query_pos_ref, key_limit_ref,
                     query_cos_ref, query_sin_ref, key_cos_ref, key_sin_ref, query_ref, *refs):
    slot_refs = refs[:n_slots]
    if project:
        weight_hbm, out_ref, peer_out_ref, weight_ref, copy_sem = refs[n_slots:]
        group = query_ref.shape[1] // heads_kv
        part = weight_ref.shape[1]
        copies = [
            pltpu.make_async_copy(
                weight_hbm.at[pl.ds(h * group, group), pl.ds(pl.multiple_of(peer_ref[0] * part, part), part)],
                weight_ref.at[pl.ds(h * group, group), :],
                copy_sem.at[h],
            )
            for h in range(heads_kv)
        ]
        for copy in copies:
            copy.start()
    else:
        (out_ref,) = refs[n_slots:]
    allowed = key_limit_ref[...] <= query_pos_ref[...]
    heads_here = query_ref.shape[1] // HEAD_SIZE // heads_kv

    def body(use):
        total = None
        for h in range(heads_kv):
            head = slice(h * HEAD_SIZE, (h + 1) * HEAD_SIZE)
            keys = turn(jnp.concatenate([slot_refs[j][0, :, head] for j in use], axis=0),
                        key_cos_ref[...], key_sin_ref[...])
            values = jnp.concatenate([slot_refs[j][1, :, head] for j in use], axis=0)
            for g in range(heads_here):
                q = h * heads_here + g
                columns = slice(q * HEAD_SIZE, (q + 1) * HEAD_SIZE)
                query = turn(query_ref[:, columns], query_cos_ref[...], query_sin_ref[...])
                scores = lax.dot_general(
                    query, keys, (((1,), (1,)), ((), ())), preferred_element_type=jnp.float32
                ) * (1.0 / math.sqrt(HEAD_SIZE))
                scores = jnp.where(allowed, scores, -1e30)
                highest = jnp.max(scores, axis=1, keepdims=True)
                weights = jnp.exp(scores - highest)
                totals = jnp.sum(weights, axis=1, keepdims=True)
                summed = jnp.dot(weights.astype(jnp.bfloat16), values, preferred_element_type=jnp.float32)
                out_ref[:, columns] = (summed / totals).astype(out_ref.dtype)
            landing = max(heads_kv - 2, 0)
            if project and h >= landing:
                if h == landing:
                    for copy in copies:
                        copy.wait()
                for k in (range(h + 1) if h == landing else [h]):
                    rows = slice(k * group, (k + 1) * group)
                    term = jnp.dot(out_ref[:, rows], weight_ref[rows, :], preferred_element_type=jnp.float32)
                    total = term if total is None else total + term
        if project:
            peer_out_ref[...] = total.astype(peer_out_ref.dtype)

    body(uses)


def tables(positions):
    half = HEAD_SIZE // 2
    freqs = 500000.0 ** (-jnp.arange(half, dtype=jnp.float32) / half)
    angles = positions.astype(jnp.float32)[:, None] * freqs[None, :]
    cosine = jnp.cos(angles)
    sine = jnp.sin(angles)
    return jnp.concatenate([cosine, cosine], axis=1), jnp.concatenate([-sine, sine], axis=1)


def attend(query_pos, key_pos, key_limit, queries, slots, uses, heads_kv, out_weight, peer):
    rows, width = queries.shape
    n_slots = len(slots)
    count = key_pos.shape[0]
    project = out_weight is not None
    query_cos, query_sin = tables(query_pos)
    key_cos, key_sin = tables(key_pos)
    vmem = pl.BlockSpec(memory_space=pltpu.VMEM)
    smem = pl.BlockSpec(memory_space=pltpu.SMEM)
    core = (lax.axis_index("ctx") % 2).astype(jnp.int32)
    args = [peer.reshape(1), core.reshape(1), query_pos.reshape(rows, 1), key_limit, query_cos, query_sin,
            key_cos, key_sin, queries] + slots
    in_specs = [smem, smem] + [vmem] * (7 + n_slots)
    out_shape = [jax.ShapeDtypeStruct((rows, width), jnp.bfloat16)]
    out_specs = [vmem]
    scratch = []
    flops = 4 * rows * count * width
    moved = 2 * (2 * rows * width + 2 * count * heads_kv * HEAD_SIZE)
    if project:
        part = out_weight.shape[1] // 2
        args.append(out_weight)
        in_specs.append(pl.BlockSpec(memory_space=pl.ANY))
        out_shape.append(jax.ShapeDtypeStruct((rows, part), jnp.bfloat16))
        out_specs.append(vmem)
        scratch += [pltpu.VMEM((width, part), jnp.bfloat16), pltpu.SemaphoreType.DMA((heads_kv,))]
        flops += 2 * rows * width * part
        moved += 2 * (width * part + rows * part)
    return pl.pallas_call(
        functools.partial(attention_kernel, n_slots, uses, heads_kv, project),
        out_shape=out_shape,
        in_specs=in_specs,
        out_specs=out_specs,
        scratch_shapes=scratch,
        compiler_params=pltpu.CompilerParams(vmem_limit_bytes=48 * 1024 * 1024),
        cost_estimate=pl.CostEstimate(
            flops=flops, transcendentals=rows * count * width // HEAD_SIZE, bytes_accessed=moved
        ),
    )(*args)


def on_device(queries, keys, values, out_weight, group_widths, pad_tokens):
    n = lax.axis_size("ctx")
    window = n // 2
    group_index = lax.axis_index("ctx")
    rows_here = queries.shape[0]
    heads_kv = keys.shape[1] // HEAD_SIZE
    context_group = queries.shape[1] // keys.shape[1]

    slots, shift = gather_window(jnp.stack([keys, values]), n, window)

    prompt_ids = jnp.arange(group_widths.shape[0], dtype=jnp.int32)
    offsets = jnp.sum(
        jnp.where(prompt_ids[None, :] < prompt_ids[:, None], group_widths[None, :], 0), axis=1
    )
    owner = jnp.sum((offsets <= group_index).astype(jnp.int32)) - 1
    picked = prompt_ids == owner
    start = jnp.sum(jnp.where(picked, offsets, 0))
    width = jnp.sum(jnp.where(picked, group_widths, 0))
    padding = jnp.sum(jnp.where(picked, pad_tokens, 0))
    length = width * rows_here - padding
    local_rows = jnp.arange(rows_here, dtype=jnp.int32)
    query_pos = (group_index - start) * rows_here + local_rows
    key_pos = ((group_index - shift - start) * rows_here)[:, None] + local_rows[None, :]
    key_pos = key_pos.reshape(-1)

    usable = (key_pos >= 0) & (key_pos < length)
    key_limit = jnp.where(usable, key_pos, FAR * rows_here).reshape(1, -1)

    n_tp = lax.axis_size("tp")
    if n_tp == 2:
        me = lax.axis_index("tp")
        attended, peer_terms = attend(
            query_pos, key_pos, key_limit, queries, slots, list(range(len(slots))), heads_kv, out_weight, 1 - me
        )
        got = lax.ppermute(peer_terms, "tp", [(0, 1), (1, 0)])
        part = out_weight.shape[1] // 2
        own_weight = lax.dynamic_slice_in_dim(out_weight, me * part, part, 1)
        own_terms = jnp.dot(attended, own_weight, preferred_element_type=jnp.float32)
        own_terms = lax.optimization_barrier(own_terms.astype(jnp.bfloat16)).astype(jnp.float32)
        return (own_terms + got.astype(jnp.float32)).astype(jnp.bfloat16)
    (attended,) = attend(query_pos, key_pos, key_limit, queries, slots, list(range(len(slots))), heads_kv, None, jnp.int32(0))
    terms = jnp.dot(attended, out_weight, preferred_element_type=jnp.float32)
    return lax.psum_scatter(terms.astype(jnp.bfloat16), "tp", scatter_dimension=1, tiled=True)


def solution(mesh):
    return jax.shard_map(
        on_device,
        mesh=mesh,
        in_specs=(P("ctx", "tp"), P("ctx", "tp"), P("ctx", "tp"), P("tp", None), P(), P()),
        out_specs=P("ctx", "tp"),
        check_vma=False,
    )
```
